512 devices in a mesh: head: 8 (over x, core), group: 64 (over z, y).
Axes of the slice: x: 4, y: 4, z: 16, core: 2. Of those that a mesh axis runs over, the one named last changes fastest.
Arguments:
- query_proj: bfloat16 [8192, 2048], P('group', 'head'), may hold values from -6 to 6
- key_proj: bfloat16 [8192, 2048], P('group', 'head'), may hold values from -6 to 6
- value_proj: bfloat16 [8192, 4096], P('group', 'head'), may hold values from -6 to 6
- gate_proj: bfloat16 [8192, 4096], P('group', 'head'), may hold values from -6 to 6
- log_decay: float32 [8192, 8], P('group', 'head'), may hold values from -0.75 to 0
- out_weight: bfloat16 [4096, 2048], P('head'), may hold values from -0.09375 to 0.09375
- residual: bfloat16 [64, 128, 2048], P('group', 'head'), may hold values from -30 to 30
- norm_gain: float32 [2048], replicated, may hold values from 0.5 to 1.5
- vocab_weight: bfloat16 [49152, 2048], P(('head', 'group')), may hold values from -2 to 2
- targets: int32 [64, 128], P('group', 'head'), may hold values from 0 to 49151
- ref_logp: float32 [64, 128], P('group', 'head'), may hold values from -16 to -1
- response_mask: int32 [64, 128], P('group', 'head'), may hold values 0 or 1
- seq_lengths: int32 [32], replicated, may hold values from 1 to 4096, 8192 in all
Outputs:
- seq_ratio: float32 [32], replicated
- state_norms: float32 [64, 8], P('group', 'head')
- max_logits: float32 [64, 128], P('group', 'head')
The draws below stay inside these ranges and needn't reach their ends.
Inputs may be any that keep to these rules, and one draw needn't show every extreme that they name: `seq_lengths`: the sequences lie end to end in order from position 0, the lengths summing to 8192.
All inputs are finite; a program needn't handle non-finite values. No bound on the sum of `response_mask` on one device may be relied on, other than what follows from the above.
Results may differ from the reference program's by a relative error of at most 0.00093.
Values may be sent and summed in bfloat16 or wider, within the bound.
No kernel may reach another device: no remote copies, remote signals or barrier semaphores. Data moves between devices by JAX's collectives and lax.ppermute only.
A program may use at most 192 MiB of HBM per device.

```python
import math
import jax
import jax.numpy as jnp
import numpy as np
from jax import lax

D = 2048
RETENTION_HEADS = 8
KD = 256
VD = 512
T_DEV = 128
NBLK = 64
STREAM_TOKENS = 8192
NSEQ = 32
VOCAB = 49152


def draw_log_decay(key, part):
    head_key = jax.random.fold_in(key, 21)
    block_key = jax.random.fold_in(key, 22)
    jitter_key = jax.random.fold_in(key, 23)
    episode_random_key = jax.random.fold_in(key, 24)
    loss_random_key = jax.random.fold_in(key, 25)
    slow_share = 0.5
    jitter = jax.random.uniform(jitter_key, (STREAM_TOKENS, RETENTION_HEADS), minval=0.5, maxval=1.5)
    slowest_head = jax.random.uniform(head_key, (RETENTION_HEADS,)) < slow_share
    block_rows = jnp.arange(STREAM_TOKENS) // T_DEV
    block_factor = jnp.exp(jax.random.uniform(block_key, (NBLK, RETENTION_HEADS), minval=math.log(0.5), maxval=0.0))[block_rows]
    base_rate = jnp.where(slowest_head, 1.5 / (STREAM_TOKENS // 2), 1.0 / 40.0)
    decay_rates_all = base_rate[None, :] * block_factor * jitter
    episodes = jax.random.uniform(episode_random_key, (STREAM_TOKENS, RETENTION_HEADS)) < 6.0 / STREAM_TOKENS
    episode_loss = jnp.log(jax.random.uniform(loss_random_key, (STREAM_TOKENS, RETENTION_HEADS), minval=0.5, maxval=0.8))
    value_output_rows = -decay_rates_all + jnp.where(episodes & slowest_head[None, :], episode_loss, 0.0)
    return value_output_rows.astype(jnp.float32)


def draw_residual(key, part):
    base = jax.random.normal(jax.random.fold_in(key, 31), (NBLK, T_DEV, D), jnp.float32)
    value_output_rows = base
    return jnp.clip(value_output_rows, -30.0, 30.0).astype(jnp.bfloat16)


def draw_vocab_weight(key, part):
    row_scale = jnp.exp(jax.random.uniform(jax.random.fold_in(key, 41), (VOCAB, 1), minval=0.0, maxval=math.log(10.0)))
    noise = jax.random.normal(jax.random.fold_in(key, 42), (VOCAB, D), jnp.float32)
    weights = noise * row_scale / math.sqrt(D)
    return jnp.clip(weights, -2.0, 2.0).astype(jnp.bfloat16)


def set_ends(entries, stream_key, least, high):
    shape = entries.shape
    spot = [jax.random.randint(jax.random.fold_in(stream_key, axis), (), 0, shape[axis]) for axis in range(len(shape))]
    entries = entries.at[tuple(spot)].set(least)
    longest = shape.index(max(shape))
    spot[longest] = (spot[longest] + 1) % shape[longest]
    return entries.at[tuple(spot)].set(high)


def levels(rng, dims, pieces, low, top_value):
    def one(axis_at, shards_of):
        draws = jax.random.uniform(jax.random.fold_in(jax.random.fold_in(rng, 6), axis_at), (shards_of,), jnp.float32, low / len(pieces), top_value / len(pieces))
        return jnp.repeat(jnp.exp(draws), dims[axis_at] // shards_of).reshape((-1,) + (1,) * (len(dims) - axis_at - 1))

    loudness = one(*pieces[0])
    for cut in pieces[1:]:
        loudness = loudness * one(*cut)
    return loudness


def rank_bounds(count, lean):
    portions = [(1 << 20) // math.isqrt(rank ** lean) + 1 for rank in range(1, count + 1)]
    scale = 1 + sum(portions) // (1 << 30)
    return np.cumsum(np.array([max(1, weight // scale) for weight in portions]))


def ranked(rng, shape, amount, skew):
    table = rank_bounds(amount, skew)
    ticket = jax.random.randint(jax.random.fold_in(rng, 1), shape, 0, int(table[amount - 1]))
    rank = jnp.searchsorted(jnp.asarray(table, jnp.int32), ticket, side="right")
    return jax.random.permutation(jax.random.fold_in(rng, 2), amount)[rank].astype(jnp.int32)


def split_up(count, total, reach, lean):
    loads = [(1 << 20) // math.isqrt(grade ** lean) + 1 for grade in range(2, count + 1)]
    spare, given = total - reach - (count - 1), [1] * (count - 1)
    while spare > 0:
        candidates = [i for i in range(count - 1) if given[i] < reach]
        mass, left = sum([loads[i] for i in candidates]), spare
        for i in candidates:
            more = min(reach - given[i], max(1, left * loads[i] // mass), spare)
            given[i] = given[i] + more
            spare = spare - more
    return np.array([reach] + given)


def ragged(own_key, count, total, limit, slope):
    if count == 2:
        one = jax.random.randint(own_key, (), max(1, total - limit), min(limit, total - 1) + 1)
        return jnp.stack([one, total - one])
    tallies = jnp.asarray(split_up(count, total, limit, slope), jnp.int32)
    pairs = (count - 1) // 2
    giver, receiver = tallies[1:1 + 2 * pairs:2], tallies[2:2 + 2 * pairs:2]
    room = jnp.minimum(giver - 1, limit - receiver)
    passed = jax.random.randint(jax.random.fold_in(own_key, 1), (pairs,), 0, 1 << 20) % (room + 1)
    tallies = tallies.at[1:1 + 2 * pairs:2].set(giver - passed).at[2:2 + 2 * pairs:2].set(receiver + passed)
    return tallies[jax.random.permutation(jax.random.fold_in(own_key, 2), count)]


def gaussian(key, dims, width, bound, cuts=(), held_as=jnp.bfloat16):
    drawn = width * jax.random.normal(key, dims, jnp.float32)
    if cuts:
        drawn = drawn * levels(key, dims, cuts, -0.22, 0.18)
    return jnp.clip(drawn, -bound, bound).astype(held_as)


def setup_inputs(seed: int = 0) -> dict:
    key_of = jax.random.split(jax.random.key(seed), 14)
    return {
        "query_proj": gaussian(key_of[0], (STREAM_TOKENS, RETENTION_HEADS * KD), 1.0, 6.0, ((0, 64), (1, 8))),
        "key_proj": gaussian(key_of[1], (STREAM_TOKENS, RETENTION_HEADS * KD), 1.0, 6.0, ((0, 64), (1, 8))),
        "value_proj": gaussian(key_of[2], (STREAM_TOKENS, RETENTION_HEADS * VD), 1.0, 6.0, ((0, 64), (1, 8))),
        "gate_proj": gaussian(key_of[3], (STREAM_TOKENS, RETENTION_HEADS * VD), 1.0, 6.0, ((0, 64), (1, 8))),
        "log_decay": draw_log_decay(jax.random.fold_in(key_of[13], 71), 0),
        "out_weight": gaussian(key_of[5], (RETENTION_HEADS * VD, D), (RETENTION_HEADS * VD) ** -0.5, 0.09375, ((0, 8),)),
        "residual": draw_residual(jax.random.fold_in(key_of[13], 71), 0),
        "norm_gain": jnp.clip(1.0 + 0.1 * jax.random.normal(key_of[7], (D,), jnp.float32), 0.5, 1.5),
        "vocab_weight": draw_vocab_weight(jax.random.fold_in(key_of[13], 71), 0),
        "targets": set_ends(ranked(key_of[9], (NBLK, T_DEV), VOCAB, 2), jax.random.fold_in(key_of[9], 3), 0, VOCAB - 1).astype(jnp.int32),
        "ref_logp": jnp.clip(-16.0 + 15.0 * jax.random.uniform(key_of[10], (NBLK, T_DEV), jnp.float32) ** levels(key_of[10], (NBLK, T_DEV), ((0, 64), (1, 8)), -0.2, 0.2), -16.0, -1.0),
        "response_mask": set_ends((jax.random.randint(key_of[11], (NBLK, T_DEV), 0, 4) < 3).astype(jnp.int32), jax.random.fold_in(key_of[11], 1), 0, 1),
        "seq_lengths": ragged(key_of[12], NSEQ, STREAM_TOKENS, STREAM_TOKENS // 2, 2).astype(jnp.int32),
    }


def layer_norm(stream, width_eps):
    mean_val = lax.optimization_barrier(jnp.mean(stream, axis=-1, keepdims=True))
    centered = stream - mean_val
    var_val = lax.optimization_barrier(jnp.mean(centered * centered, axis=-1, keepdims=True))
    return centered / jnp.sqrt(var_val + width_eps)

def reference(query_proj, key_proj, value_proj, gate_proj, log_decay, out_weight, residual, norm_gain, vocab_weight, targets, ref_logp, response_mask, seq_lengths):
    highest_precision = lax.Precision.HIGHEST
    starts = jnp.cumsum(seq_lengths) - seq_lengths
    positions = jnp.arange(STREAM_TOKENS, dtype=jnp.int32)
    seq_ids = lax.optimization_barrier(jnp.sum((positions[:, None] >= starts[None, 1:]).astype(jnp.int32), axis=1)).astype(jnp.int32)
    is_start = jnp.any(positions[:, None] == starts[None, :], axis=1)
    key_scaling = KD ** (-0.5)
    local_pos = jnp.arange(T_DEV, dtype=jnp.int32)
    vocab_cols = vocab_weight.T

    def block_step(carried_state, inputs):
        query_blk, key_blk, value_blk, gate_blk, decay_blk, seq_blk, start_blk, resid_blk, target_blk = inputs
        cumulative_decay = jnp.cumsum(decay_blk, axis=0)
        same_seq = (seq_blk[:, None] == seq_blk[None, :]) & (local_pos[None, :] <= local_pos[:, None])
        gap_log = cumulative_decay[:, None, :] - cumulative_decay[None, :, :]
        decay_mat = jnp.where(same_seq[:, :, None], jnp.exp(jnp.minimum(gap_log, 0.0)), 0.0)
        query_in_float = query_blk.astype(jnp.float32)
        key_in_float = key_blk.astype(jnp.float32)
        value_in_float = value_blk.astype(jnp.float32)
        raw_scores = jnp.einsum('thd,shd->tsh', query_in_float, key_in_float)
        weights_in = (raw_scores * key_scaling * decay_mat).astype(jnp.bfloat16)
        in_block = jnp.einsum('tsh,shv->thv', weights_in.astype(jnp.float32), value_in_float)
        continuation_flags = (seq_blk == seq_blk[0]) & jnp.logical_not(start_blk[0])
        state_contribution = jnp.einsum('ugo,gow->ugw', query_in_float, carried_state, precision=highest_precision) * key_scaling * (jnp.exp(cumulative_decay) * continuation_flags[:, None].astype(jnp.float32))[:, :, None]
        retained = in_block + state_contribution
        norm_out = jnp.log(1.0 + jnp.sqrt(lax.optimization_barrier(jnp.mean(carried_state * carried_state, axis=(1, 2))) + 1e-06))
        final_decay_weight = jnp.where((seq_blk == seq_blk[-1])[:, None], jnp.exp(cumulative_decay[-1][None, :] - cumulative_decay), 0.0)
        block_total_sum = jnp.einsum('ane,anl->nel', key_in_float * final_decay_weight[:, :, None], value_in_float, precision=highest_precision)
        block_decay = jnp.where(jnp.all(continuation_flags), jnp.exp(cumulative_decay[-1]), 0.0)
        new_state = block_decay[:, None, None] * carried_state + block_total_sum
        normed = layer_norm(retained, 1e-06)
        gated_out = (normed * jax.nn.silu(gate_blk.astype(jnp.float32))).astype(jnp.bfloat16).reshape(T_DEV, RETENTION_HEADS * VD)
        stream = resid_blk.astype(jnp.float32) + jnp.dot(gated_out, out_weight, preferred_element_type=jnp.float32)
        hidden = (layer_norm(stream, 1e-05) * norm_gain).astype(jnp.bfloat16)
        logits = jnp.dot(hidden, vocab_cols, preferred_element_type=jnp.float32)
        top = lax.optimization_barrier(jnp.max(logits, axis=1))
        exp_total = lax.optimization_barrier(jnp.sum(jnp.exp(logits - top[:, None]), axis=1))
        picked = jnp.take_along_axis(logits, target_blk[:, None], axis=1)[:, 0]
        token_logp = picked - top - jnp.log(exp_total)
        return (new_state, (norm_out, top, token_logp))
    inputs = (query_proj.reshape(NBLK, T_DEV, RETENTION_HEADS, KD), key_proj.reshape(NBLK, T_DEV, RETENTION_HEADS, KD), value_proj.reshape(NBLK, T_DEV, RETENTION_HEADS, VD), gate_proj.reshape(NBLK, T_DEV, RETENTION_HEADS, VD), log_decay.reshape(NBLK, T_DEV, RETENTION_HEADS), seq_ids.reshape(NBLK, T_DEV), is_start.reshape(NBLK, T_DEV), residual, targets)
    initial = jnp.zeros((RETENTION_HEADS, KD, VD), jnp.float32)
    final_state, outputs = lax.scan(block_step, initial, inputs)
    state_norms, max_logits, token_logp = outputs
    token_ratio = response_mask.astype(jnp.float32) * (token_logp - ref_logp)
    seq_total = jax.ops.segment_sum(token_ratio.reshape(-1), seq_ids, num_segments=NSEQ)
    seq_ratio = seq_total / seq_lengths.astype(jnp.float32)
    return (seq_ratio, state_norms, max_logits)
```

```python
import jax
import jax.numpy as jnp
from jax import lax
from jax.sharding import PartitionSpec as P


def layer_norm(stream, width_eps):
    mean_val = jnp.mean(stream, axis=-1, keepdims=True)
    centered = stream - mean_val
    var_val = jnp.mean(centered * centered, axis=-1, keepdims=True)
    return centered / jnp.sqrt(var_val + width_eps)


def per_device(
    query_proj,
    key_proj,
    value_proj,
    gate_proj,
    log_decay,
    out_weight,
    residual,
    norm_gain,
    vocab_weight,
    targets,
    ref_logp,
    response_mask,
    seq_lengths,
):
    highest_precision = lax.Precision.HIGHEST
    head_count = lax.axis_size("head")
    group_count = lax.axis_size("group")
    head_index = lax.axis_index("head")
    group_index = lax.axis_index("group")
    tok_count = query_proj.shape[0]
    heads_here = log_decay.shape[1]
    key_width = query_proj.shape[1] // heads_here
    value_width = value_proj.shape[1] // heads_here
    slice_rows = residual.shape[1]
    seq_count = seq_lengths.shape[0]
    vocab_here = vocab_weight.shape[0]
    key_scaling = key_width ** (-0.5)
    starts = jnp.cumsum(seq_lengths) - seq_lengths
    local_pos = jnp.arange(tok_count, dtype=jnp.int32)
    positions = group_index * tok_count + local_pos
    seq_ids = jnp.sum((positions[:, None] >= starts[None, 1:]).astype(jnp.int32), axis=1)
    is_start = jnp.any(positions[:, None] == starts[None, :], axis=1)
    cumulative_decay = jnp.cumsum(log_decay, axis=0)
    same_seq = (seq_ids[:, None] == seq_ids[None, :]) & (local_pos[None, :] <= local_pos[:, None])
    gap_log = cumulative_decay[:, None, :] - cumulative_decay[None, :, :]
    decay_mat = jnp.where(same_seq[:, :, None], jnp.exp(jnp.minimum(gap_log, 0.0)), 0.0)
    query_heads = query_proj.reshape(tok_count, heads_here, key_width)
    key_heads = key_proj.reshape(tok_count, heads_here, key_width)
    value_heads = value_proj.reshape(tok_count, heads_here, value_width)
    raw_scores = jnp.einsum(
        "thd,shd->tsh", query_heads, key_heads, preferred_element_type=jnp.float32
    )
    weights_in = (raw_scores * key_scaling * decay_mat).astype(jnp.bfloat16)
    in_block = jnp.einsum(
        "tsh,shv->thv", weights_in, value_heads, preferred_element_type=jnp.float32
    )
    continuation_flags = (seq_ids == seq_ids[0]) & jnp.logical_not(is_start[0])
    final_decay_weight = jnp.where(
        (seq_ids == seq_ids[-1])[:, None],
        jnp.exp(cumulative_decay[-1][None, :] - cumulative_decay),
        0.0,
    )
    key_as_float = key_heads.astype(jnp.float32)
    value_as_float = value_heads.astype(jnp.float32)
    block_total_sum = jnp.einsum(
        "ane,anl->nel",
        key_as_float * final_decay_weight[:, :, None],
        value_as_float,
        precision=highest_precision,
    )
    block_decay = jnp.where(jnp.all(continuation_flags), jnp.exp(cumulative_decay[-1]), 0.0)

    assert heads_here == 1
    chunk = key_width * value_width // group_count
    extras = jnp.concatenate(
        [
            block_decay,
            targets[0].astype(jnp.float32),
            ref_logp[0],
            response_mask[0].astype(jnp.float32),
        ]
    )
    extra_width = 128 * pl_cdiv(extras.shape[0], 128)
    extras = jnp.pad(extras, (0, extra_width - extras.shape[0]))
    payload = jnp.concatenate(
        [
            block_total_sum.reshape(group_count, chunk),
            jnp.broadcast_to(extras[None, :], (group_count, extra_width)),
        ],
        axis=1,
    )
    received = lax.all_to_all(payload, "group", 0, 0, tiled=True)
    slices_in = received[:, :chunk]
    decay_all = received[:, chunk]
    targets_all = received[:, chunk + 1 : chunk + 1 + slice_rows].astype(jnp.int32)
    ref_all = received[:, chunk + 1 + slice_rows : chunk + 1 + 2 * slice_rows]
    mask_all = received[:, chunk + 1 + 2 * slice_rows : chunk + 1 + 3 * slice_rows]
    blk = jnp.arange(group_count, dtype=jnp.int32)
    between = (blk[None, None, :] > blk[None, :, None]) & (blk[None, None, :] < blk[:, None, None])
    weights = jnp.prod(jnp.where(between, decay_all[None, None, :], 1.0), axis=2)
    weights = jnp.where(blk[None, :] < blk[:, None], weights, 0.0)
    slices_out = jnp.dot(weights, slices_in, precision=highest_precision)
    carried_state = lax.all_to_all(slices_out, "group", 0, 0, tiled=True).reshape(
        heads_here, key_width, value_width
    )

    query_as_float = query_heads.astype(jnp.float32)
    state_contribution = (
        jnp.einsum("ugo,gow->ugw", query_as_float, carried_state, precision=highest_precision)
        * key_scaling
        * (jnp.exp(cumulative_decay) * continuation_flags[:, None].astype(jnp.float32))[:, :, None]
    )
    retained = in_block + state_contribution
    state_norms = jnp.log(
        1.0 + jnp.sqrt(jnp.mean(carried_state * carried_state, axis=(1, 2)) + 1e-06)
    )[None, :]
    normed = layer_norm(retained, 1e-06)
    gate_float = gate_proj.reshape(tok_count, heads_here, value_width).astype(jnp.float32)
    gated_out = (
        (normed * jax.nn.silu(gate_float))
        .astype(jnp.bfloat16)
        .reshape(tok_count, heads_here * value_width)
    )
    own_branch = lax.psum_scatter(
        jnp.dot(gated_out, out_weight, preferred_element_type=jnp.float32),
        "head",
        scatter_dimension=0,
        tiled=True,
    )
    stream = residual[0].astype(jnp.float32) + own_branch
    hidden = (layer_norm(stream, 1e-05) * norm_gain).astype(jnp.bfloat16)
    vocab_rows = lax.all_gather(vocab_weight, "head", axis=0, tiled=True)
    entry_ids = (
        (jnp.arange(head_count, dtype=jnp.int32)[:, None] * group_count + group_index) * vocab_here
        + jnp.arange(vocab_here, dtype=jnp.int32)[None, :]
    ).reshape(-1)
    all_targets = targets_all.reshape(-1)
    logits = lax.dot_general(
        lax.all_gather(hidden, "group", axis=0, tiled=True),
        vocab_rows,
        (((1,), (1,)), ((), ())),
        preferred_element_type=jnp.float32,
    )
    top = jnp.max(logits, axis=1)
    exp_total = jnp.sum(jnp.exp(logits - top[:, None]), axis=1)
    picked = jnp.sum(jnp.where(entry_ids[None, :] == all_targets[:, None], logits, 0.0), axis=1)
    stats = lax.all_gather(jnp.stack([top, exp_total, picked]), "group")
    merged_max = jnp.max(stats[:, 0], axis=0)
    merged_total = jnp.sum(stats[:, 1] * jnp.exp(stats[:, 0] - merged_max[None, :]), axis=0)
    merged_target = jnp.sum(stats[:, 2], axis=0)
    token_logp = merged_target - merged_max - jnp.log(merged_total)
    token_ratio = mask_all.reshape(-1) * (token_logp - ref_all.reshape(-1))
    own_max = lax.dynamic_slice_in_dim(merged_max, group_index * slice_rows, slice_rows, 0)
    token_positions = (
        blk[:, None] * tok_count
        + head_index * slice_rows
        + jnp.arange(slice_rows, dtype=jnp.int32)[None, :]
    ).reshape(-1)
    token_seq = jnp.sum((token_positions[:, None] >= starts[None, 1:]).astype(jnp.int32), axis=1)
    member = (token_seq[:, None] == jnp.arange(seq_count, dtype=jnp.int32)[None, :]).astype(
        jnp.float32
    )
    partial_sums = jnp.sum(member * token_ratio[:, None], axis=0)
    seq_total = lax.psum(partial_sums, "head")
    seq_ratio = seq_total / seq_lengths.astype(jnp.float32)
    return (seq_ratio, state_norms, own_max[None, :])


def pl_cdiv(a, b):
    return (a + b - 1) // b


def solution(mesh):
    placed = (
        P("group", "head"),
        P("group", "head"),
        P("group", "head"),
        P("group", "head"),
        P("group", "head"),
        P("head", None),
        P("group", "head", None),
        P(),
        P(("head", "group"), None),
        P("group", "head"),
        P("group", "head"),
        P("group", "head"),
        P(),
    )
    return jax.shard_map(
        per_device,
        mesh=mesh,
        in_specs=placed,
        out_specs=(P(), P("group", "head"), P("group", "head")),
        check_vma=False,
    )
```

```python
import jax
import jax.numpy as jnp
from jax import lax
from jax.sharding import PartitionSpec as P


def layer_norm(stream, width_eps):
    mean_val = jnp.mean(stream, axis=-1, keepdims=True)
    centered = stream - mean_val
    var_val = jnp.mean(centered * centered, axis=-1, keepdims=True)
    return centered / jnp.sqrt(var_val + width_eps)


def per_device(
    query_proj,
    key_proj,
    value_proj,
    gate_proj,
    log_decay,
    out_weight,
    residual,
    norm_gain,
    vocab_weight,
    targets,
    ref_logp,
    response_mask,
    seq_lengths,
):
    highest_precision = lax.Precision.HIGHEST
    head_count = lax.axis_size("head")
    group_count = lax.axis_size(("ga", "gb"))
    head_index = lax.axis_index("head")
    group_index = lax.axis_index(("ga", "gb"))
    tok_count = query_proj.shape[0]
    heads_here = log_decay.shape[1]
    key_width = query_proj.shape[1] // heads_here
    value_width = value_proj.shape[1] // heads_here
    slice_rows = residual.shape[1]
    seq_count = seq_lengths.shape[0]
    vocab_here = vocab_weight.shape[0]
    key_scaling = key_width ** (-0.5)
    starts = jnp.cumsum(seq_lengths) - seq_lengths
    local_pos = jnp.arange(tok_count, dtype=jnp.int32)
    positions = group_index * tok_count + local_pos
    seq_ids = jnp.sum((positions[:, None] >= starts[None, 1:]).astype(jnp.int32), axis=1)
    is_start = jnp.any(positions[:, None] == starts[None, :], axis=1)
    cumulative_decay = jnp.cumsum(log_decay, axis=0)
    same_seq = (seq_ids[:, None] == seq_ids[None, :]) & (local_pos[None, :] <= local_pos[:, None])
    gap_log = cumulative_decay[:, None, :] - cumulative_decay[None, :, :]
    decay_mat = jnp.where(same_seq[:, :, None], jnp.exp(jnp.minimum(gap_log, 0.0)), 0.0)
    query_heads = query_proj.reshape(tok_count, heads_here, key_width)
    key_heads = key_proj.reshape(tok_count, heads_here, key_width)
    value_heads = value_proj.reshape(tok_count, heads_here, value_width)
    raw_scores = jnp.einsum(
        "thd,shd->tsh", query_heads, key_heads, preferred_element_type=jnp.float32
    )
    weights_in = (raw_scores * key_scaling * decay_mat).astype(jnp.bfloat16)
    in_block = jnp.einsum(
        "tsh,shv->thv", weights_in, value_heads, preferred_element_type=jnp.float32
    )
    continuation_flags = (seq_ids == seq_ids[0]) & jnp.logical_not(is_start[0])
    final_decay_weight = jnp.where(
        (seq_ids == seq_ids[-1])[:, None],
        jnp.exp(cumulative_decay[-1][None, :] - cumulative_decay),
        0.0,
    )
    key_as_float = key_heads.astype(jnp.float32)
    value_as_float = value_heads.astype(jnp.float32)
    block_total_sum = jnp.einsum(
        "ane,anl->nel",
        key_as_float * final_decay_weight[:, :, None],
        value_as_float,
        precision=highest_precision,
    )
    block_decay = jnp.where(jnp.all(continuation_flags), jnp.exp(cumulative_decay[-1]), 0.0)

    assert heads_here == 1
    chunk = key_width * value_width // group_count
    extras = block_decay
    extra_width = 128 * pl_cdiv(extras.shape[0], 128)
    extras = jnp.pad(extras, (0, extra_width - extras.shape[0]))
    payload = jnp.concatenate(
        [
            block_total_sum.reshape(group_count, chunk),
            jnp.broadcast_to(extras[None, :], (group_count, extra_width)),
        ],
        axis=1,
    )
    received = lax.all_to_all(payload, ("ga", "gb"), 0, 0, tiled=True)
    slices_in = received[:, :chunk]
    decay_all = received[:, chunk]
    blk = jnp.arange(group_count, dtype=jnp.int32)
    between = (blk[None, None, :] > blk[None, :, None]) & (blk[None, None, :] < blk[:, None, None])
    weights = jnp.prod(jnp.where(between, decay_all[None, None, :], 1.0), axis=2)
    weights = jnp.where(blk[None, :] < blk[:, None], weights, 0.0)
    slices_out = jnp.dot(weights, slices_in, precision=highest_precision)
    carried_state = lax.all_to_all(slices_out, ("ga", "gb"), 0, 0, tiled=True).reshape(
        heads_here, key_width, value_width
    )

    query_as_float = query_heads.astype(jnp.float32)
    state_contribution = (
        jnp.einsum("ugo,gow->ugw", query_as_float, carried_state, precision=highest_precision)
        * key_scaling
        * (jnp.exp(cumulative_decay) * continuation_flags[:, None].astype(jnp.float32))[:, :, None]
    )
    retained = in_block + state_contribution
    state_norms = jnp.log(
        1.0 + jnp.sqrt(jnp.mean(carried_state * carried_state, axis=(1, 2)) + 1e-06)
    )[None, :]
    normed = layer_norm(retained, 1e-06)
    gate_float = gate_proj.reshape(tok_count, heads_here, value_width).astype(jnp.float32)
    gated_out = (
        (normed * jax.nn.silu(gate_float))
        .astype(jnp.bfloat16)
        .reshape(tok_count, heads_here * value_width)
    )
    own_branch = lax.psum_scatter(
        jnp.dot(gated_out, out_weight, preferred_element_type=jnp.float32),
        "head",
        scatter_dimension=0,
        tiled=True,
    )
    stream = residual[0].astype(jnp.float32) + own_branch
    hidden = (layer_norm(stream, 1e-05) * norm_gain).astype(jnp.bfloat16)

    sub = lax.axis_size("gb")
    ga_index = lax.axis_index("ga")
    gb_index = lax.axis_index("gb")
    code = jnp.concatenate([targets[0] // 256, targets[0] % 256]).astype(jnp.bfloat16)
    code_row = jnp.pad(code, (0, hidden.shape[1] - code.shape[0]))[None, :]
    hidden_ext = jnp.concatenate([hidden, code_row], axis=0)
    gathered = lax.all_gather(lax.all_gather(hidden_ext, "head"), "gb")
    hidden_all = gathered[:, :, :slice_rows, :].reshape(-1, hidden.shape[1])
    code_all = gathered[:, :, slice_rows, : 2 * slice_rows].astype(jnp.int32)
    all_targets = (code_all[..., :slice_rows] * 256 + code_all[..., slice_rows:]).reshape(-1)
    vocab_rows = lax.all_gather(vocab_weight, "ga", axis=0, tiled=True)
    part_count = lax.axis_size("ga")
    entry_ids = (
        (
            head_index * group_count
            + jnp.arange(part_count, dtype=jnp.int32)[:, None] * sub
            + gb_index
        )
        * vocab_here
        + jnp.arange(vocab_here, dtype=jnp.int32)[None, :]
    ).reshape(-1)
    logits = lax.dot_general(
        hidden_all,
        vocab_rows,
        (((1,), (1,)), ((), ())),
        preferred_element_type=jnp.float32,
    )
    top = jnp.max(logits, axis=1)
    exp_total = jnp.sum(jnp.exp(logits - top[:, None]), axis=1)
    picked = jnp.sum(jnp.where(entry_ids[None, :] == all_targets[:, None], logits, 0.0), axis=1)
    own_mask = response_mask[0].astype(jnp.float32)
    own_positions = positions[0] + head_index * slice_rows + jnp.arange(slice_rows, dtype=jnp.int32)
    own_seq = jnp.sum((own_positions[:, None] >= starts[None, 1:]).astype(jnp.int32), axis=1)
    own_member = (own_seq[:, None] == jnp.arange(seq_count, dtype=jnp.int32)[None, :]).astype(
        jnp.float32
    )
    ref_sums = jnp.sum(own_member * (own_mask * ref_logp[0])[:, None], axis=0)
    token_count = top.shape[0]
    side = jnp.concatenate([ref_sums, own_mask])
    side = jnp.pad(side, (0, token_count - side.shape[0]))
    stats = lax.all_gather(jnp.stack([top, exp_total, picked, side]), ("head", "gb"))
    merged_max = jnp.max(stats[:, 0], axis=0)
    merged_total = jnp.sum(stats[:, 1] * jnp.exp(stats[:, 0] - merged_max[None, :]), axis=0)
    merged_target = jnp.sum(stats[:, 2], axis=0)
    token_logp = merged_target - merged_max - jnp.log(merged_total)
    class_ref = jnp.sum(stats[:, 3, :seq_count], axis=0)
    class_mask = jnp.transpose(
        stats[:, 3, seq_count : seq_count + slice_rows].reshape(head_count, sub, slice_rows),
        (1, 0, 2),
    ).reshape(-1)
    own_max = lax.dynamic_slice_in_dim(
        merged_max, (gb_index * head_count + head_index) * slice_rows, slice_rows, 0
    )
    token_positions = (
        (ga_index * sub + jnp.arange(sub, dtype=jnp.int32))[:, None] * tok_count
        + jnp.arange(tok_count, dtype=jnp.int32)[None, :]
    ).reshape(-1)
    token_seq = jnp.sum((token_positions[:, None] >= starts[None, 1:]).astype(jnp.int32), axis=1)
    member = (token_seq[:, None] == jnp.arange(seq_count, dtype=jnp.int32)[None, :]).astype(
        jnp.float32
    )
    partial_sums = jnp.sum(member * (class_mask * token_logp)[:, None], axis=0) - class_ref
    seq_total = lax.psum(partial_sums, "ga")
    seq_ratio = seq_total / seq_lengths.astype(jnp.float32)
    return (seq_ratio, state_norms, own_max[None, :])


def pl_cdiv(a, b):
    return (a + b - 1) // b


def solution(mesh):
    from jax.sharding import Mesh

    head_size, group_size = mesh.devices.shape
    sub = 8 if group_size % 8 == 0 else 1
    fine = Mesh(
        mesh.devices.reshape(head_size, group_size // sub, sub), ("head", "ga", "gb")
    )
    group = ("ga", "gb")
    placed = (
        P(group, "head"),
        P(group, "head"),
        P(group, "head"),
        P(group, "head"),
        P(group, "head"),
        P("head", None),
        P(group, "head", None),
        P(),
        P(("head", "ga", "gb"), None),
        P(group, "head"),
        P(group, "head"),
        P(group, "head"),
        P(),
    )
    return jax.shard_map(
        per_device,
        mesh=fine,
        in_specs=placed,
        out_specs=(P(), P(group, "head"), P(group, "head")),
        check_vma=False,
    )
```

```python
import jax
import jax.numpy as jnp
from jax import lax
from jax.sharding import PartitionSpec as P


def layer_norm(stream, width_eps):
    mean_val = jnp.mean(stream, axis=-1, keepdims=True)
    centered = stream - mean_val
    var_val = jnp.mean(centered * centered, axis=-1, keepdims=True)
    return centered / jnp.sqrt(var_val + width_eps)


def per_device(
    query_proj,
    key_proj,
    value_proj,
    gate_proj,
    log_decay,
    out_weight,
    residual,
    norm_gain,
    vocab_weight,
    targets,
    ref_logp,
    response_mask,
    seq_lengths,
):
    highest_precision = lax.Precision.HIGHEST
    head_count = lax.axis_size("head")
    group_count = lax.axis_size(("ga", "gb"))
    head_index = lax.axis_index("head")
    group_index = lax.axis_index(("ga", "gb"))
    tok_count = query_proj.shape[0]
    heads_here = log_decay.shape[1]
    key_width = query_proj.shape[1] // heads_here
    value_width = value_proj.shape[1] // heads_here
    slice_rows = residual.shape[1]
    seq_count = seq_lengths.shape[0]
    vocab_here = vocab_weight.shape[0]
    key_scaling = key_width ** (-0.5)
    starts = jnp.cumsum(seq_lengths) - seq_lengths
    local_pos = jnp.arange(tok_count, dtype=jnp.int32)
    positions = group_index * tok_count + local_pos
    seq_ids = jnp.sum((positions[:, None] >= starts[None, 1:]).astype(jnp.int32), axis=1)
    is_start = jnp.any(positions[:, None] == starts[None, :], axis=1)
    cumulative_decay = jnp.cumsum(log_decay, axis=0)
    same_seq = (seq_ids[:, None] == seq_ids[None, :]) & (local_pos[None, :] <= local_pos[:, None])
    gap_log = cumulative_decay[:, None, :] - cumulative_decay[None, :, :]
    decay_mat = jnp.where(same_seq[:, :, None], jnp.exp(jnp.minimum(gap_log, 0.0)), 0.0)
    query_heads = query_proj.reshape(tok_count, heads_here, key_width)
    key_heads = key_proj.reshape(tok_count, heads_here, key_width)
    value_heads = value_proj.reshape(tok_count, heads_here, value_width)
    raw_scores = jnp.einsum(
        "thd,shd->tsh", query_heads, key_heads, preferred_element_type=jnp.float32
    )
    weights_in = (raw_scores * key_scaling * decay_mat).astype(jnp.bfloat16)
    in_block = jnp.einsum(
        "tsh,shv->thv", weights_in, value_heads, preferred_element_type=jnp.float32
    )
    continuation_flags = (seq_ids == seq_ids[0]) & jnp.logical_not(is_start[0])
    final_decay_weight = jnp.where(
        (seq_ids == seq_ids[-1])[:, None],
        jnp.exp(cumulative_decay[-1][None, :] - cumulative_decay),
        0.0,
    )
    key_as_float = key_heads.astype(jnp.float32)
    value_as_float = value_heads.astype(jnp.float32)
    block_total_sum = jnp.einsum(
        "ane,anl->nel",
        key_as_float * final_decay_weight[:, :, None],
        value_as_float,
        precision=highest_precision,
    )
    block_decay = jnp.where(jnp.all(continuation_flags), jnp.exp(cumulative_decay[-1]), 0.0)

    assert heads_here == 1
    chunk = key_width * value_width // group_count
    extras = block_decay
    extra_width = 128 * pl_cdiv(extras.shape[0], 128)
    extras = jnp.pad(extras, (0, extra_width - extras.shape[0]))
    payload = jnp.concatenate(
        [
            block_total_sum.reshape(group_count, chunk),
            jnp.broadcast_to(extras[None, :], (group_count, extra_width)),
        ],
        axis=1,
    )
    received = lax.all_to_all(payload, ("ga", "gb"), 0, 0, tiled=True)
    slices_in = received[:, :chunk]
    decay_all = received[:, chunk]
    blk = jnp.arange(group_count, dtype=jnp.int32)
    between = (blk[None, None, :] > blk[None, :, None]) & (blk[None, None, :] < blk[:, None, None])
    weights = jnp.prod(jnp.where(between, decay_all[None, None, :], 1.0), axis=2)
    weights = jnp.where(blk[None, :] < blk[:, None], weights, 0.0)
    slices_out = jnp.dot(weights, slices_in, precision=highest_precision)
    carried_state = lax.all_to_all(slices_out, ("ga", "gb"), 0, 0, tiled=True).reshape(
        heads_here, key_width, value_width
    )

    vocab_rows = lax.all_gather(vocab_weight, "ga", axis=0, tiled=True)
    vocab_rows, carried_state = lax.optimization_barrier((vocab_rows, carried_state))
    query_as_float = query_heads.astype(jnp.float32)
    state_contribution = (
        jnp.einsum("ugo,gow->ugw", query_as_float, carried_state, precision=highest_precision)
        * key_scaling
        * (jnp.exp(cumulative_decay) * continuation_flags[:, None].astype(jnp.float32))[:, :, None]
    )
    retained = in_block + state_contribution
    state_norms = jnp.log(
        1.0 + jnp.sqrt(jnp.mean(carried_state * carried_state, axis=(1, 2)) + 1e-06)
    )[None, :]
    normed = layer_norm(retained, 1e-06)
    gate_float = gate_proj.reshape(tok_count, heads_here, value_width).astype(jnp.float32)
    gated_out = (
        (normed * jax.nn.silu(gate_float))
        .astype(jnp.bfloat16)
        .reshape(tok_count, heads_here * value_width)
    )
    own_branch = lax.psum_scatter(
        jnp.dot(gated_out, out_weight, preferred_element_type=jnp.float32),
        "head",
        scatter_dimension=0,
        tiled=True,
    )
    stream = residual[0].astype(jnp.float32) + own_branch
    hidden = (layer_norm(stream, 1e-05) * norm_gain).astype(jnp.bfloat16)

    sub = lax.axis_size("gb")
    ga_index = lax.axis_index("ga")
    gb_index = lax.axis_index("gb")
    code = jnp.concatenate([targets[0] // 256, targets[0] % 256]).astype(jnp.bfloat16)
    code_row = jnp.pad(code, (0, hidden.shape[1] - code.shape[0]))[None, :]
    hidden_ext = jnp.concatenate([hidden, code_row], axis=0)
    gathered = lax.all_gather(lax.all_gather(hidden_ext, "head"), "gb")
    hidden_all = gathered[:, :, :slice_rows, :].reshape(-1, hidden.shape[1])
    code_all = gathered[:, :, slice_rows, : 2 * slice_rows].astype(jnp.int32)
    all_targets = (code_all[..., :slice_rows] * 256 + code_all[..., slice_rows:]).reshape(-1)
    part_count = lax.axis_size("ga")
    entry_ids = (
        (
            head_index * group_count
            + jnp.arange(part_count, dtype=jnp.int32)[:, None] * sub
            + gb_index
        )
        * vocab_here
        + jnp.arange(vocab_here, dtype=jnp.int32)[None, :]
    ).reshape(-1)
    logits = lax.dot_general(
        hidden_all,
        vocab_rows,
        (((1,), (1,)), ((), ())),
        preferred_element_type=jnp.float32,
    )
    top = jnp.max(logits, axis=1)
    exp_total = jnp.sum(jnp.exp(logits - top[:, None]), axis=1)
    picked = jnp.sum(jnp.where(entry_ids[None, :] == all_targets[:, None], logits, 0.0), axis=1)
    outgoing = jnp.stack([top, exp_total, picked]).reshape(3, sub, head_count, slice_rows)
    outgoing = jnp.transpose(outgoing, (2, 1, 0, 3)).reshape(head_count * sub, 3 * slice_rows)
    incoming = lax.all_to_all(outgoing, ("head", "gb"), 0, 0, tiled=True).reshape(
        head_count * sub, 3, slice_rows
    )
    own_max = jnp.max(incoming[:, 0], axis=0)
    own_total = jnp.sum(incoming[:, 1] * jnp.exp(incoming[:, 0] - own_max[None, :]), axis=0)
    own_target = jnp.sum(incoming[:, 2], axis=0)
    token_logp = own_target - own_max - jnp.log(own_total)
    token_ratio = response_mask[0].astype(jnp.float32) * (token_logp - ref_logp[0])
    own_positions = positions[0] + head_index * slice_rows + jnp.arange(slice_rows, dtype=jnp.int32)
    own_seq = jnp.sum((own_positions[:, None] >= starts[None, 1:]).astype(jnp.int32), axis=1)
    member = (own_seq[:, None] == jnp.arange(seq_count, dtype=jnp.int32)[None, :]).astype(
        jnp.float32
    )
    partial_sums = jnp.sum(member * token_ratio[:, None], axis=0)
    seq_total = lax.psum(partial_sums, ("head", "ga", "gb"))
    seq_ratio = seq_total / seq_lengths.astype(jnp.float32)
    return (seq_ratio, state_norms, own_max[None, :])


def pl_cdiv(a, b):
    return (a + b - 1) // b


def solution(mesh):
    from jax.sharding import Mesh

    head_size, group_size = mesh.devices.shape
    sub = 8 if group_size % 8 == 0 else 1
    fine = Mesh(
        mesh.devices.reshape(head_size, group_size // sub, sub), ("head", "ga", "gb")
    )
    group = ("ga", "gb")
    placed = (
        P(group, "head"),
        P(group, "head"),
        P(group, "head"),
        P(group, "head"),
        P(group, "head"),
        P("head", None),
        P(group, "head", None),
        P(),
        P(("head", "ga", "gb"), None),
        P(group, "head"),
        P(group, "head"),
        P(group, "head"),
        P(),
    )
    return jax.shard_map(
        per_device,
        mesh=fine,
        in_specs=placed,
        out_specs=(P(), P(group, "head"), P(group, "head")),
        check_vma=False,
    )
```

```python
import jax
import jax.numpy as jnp
from jax import lax
from jax.sharding import PartitionSpec as P


def layer_norm(stream, width_eps):
    mean_val = jnp.mean(stream, axis=-1, keepdims=True)
    centered = stream - mean_val
    var_val = jnp.mean(centered * centered, axis=-1, keepdims=True)
    return centered / jnp.sqrt(var_val + width_eps)


def per_device(
    query_proj,
    key_proj,
    value_proj,
    gate_proj,
    log_decay,
    out_weight,
    residual,
    norm_gain,
    vocab_weight,
    targets,
    ref_logp,
    response_mask,
    seq_lengths,
):
    highest_precision = lax.Precision.HIGHEST
    head_count = lax.axis_size("head")
    group_count = lax.axis_size(("ga", "gb"))
    head_index = lax.axis_index("head")
    group_index = lax.axis_index(("ga", "gb"))
    tok_count = query_proj.shape[0]
    heads_here = log_decay.shape[1]
    key_width = query_proj.shape[1] // heads_here
    value_width = value_proj.shape[1] // heads_here
    slice_rows = residual.shape[1]
    seq_count = seq_lengths.shape[0]
    vocab_here = vocab_weight.shape[0]
    key_scaling = key_width ** (-0.5)
    starts = jnp.cumsum(seq_lengths) - seq_lengths
    local_pos = jnp.arange(tok_count, dtype=jnp.int32)
    positions = group_index * tok_count + local_pos
    seq_ids = jnp.sum((positions[:, None] >= starts[None, 1:]).astype(jnp.int32), axis=1)
    is_start = jnp.any(positions[:, None] == starts[None, :], axis=1)
    cumulative_decay = jnp.cumsum(log_decay, axis=0)
    same_seq = (seq_ids[:, None] == seq_ids[None, :]) & (local_pos[None, :] <= local_pos[:, None])
    gap_log = cumulative_decay[:, None, :] - cumulative_decay[None, :, :]
    decay_mat = jnp.where(same_seq[:, :, None], jnp.exp(jnp.minimum(gap_log, 0.0)), 0.0)
    query_heads = query_proj.reshape(tok_count, heads_here, key_width)
    key_heads = key_proj.reshape(tok_count, heads_here, key_width)
    value_heads = value_proj.reshape(tok_count, heads_here, value_width)
    raw_scores = jnp.einsum(
        "thd,shd->tsh", query_heads, key_heads, preferred_element_type=jnp.float32
    )
    weights_in = (raw_scores * key_scaling * decay_mat).astype(jnp.bfloat16)
    in_block = jnp.einsum(
        "tsh,shv->thv", weights_in, value_heads, preferred_element_type=jnp.float32
    )
    continuation_flags = (seq_ids == seq_ids[0]) & jnp.logical_not(is_start[0])
    final_decay_weight = jnp.where(
        (seq_ids == seq_ids[-1])[:, None],
        jnp.exp(cumulative_decay[-1][None, :] - cumulative_decay),
        0.0,
    )
    key_as_float = key_heads.astype(jnp.float32)
    value_as_float = value_heads.astype(jnp.float32)
    block_total_sum = jnp.einsum(
        "ane,anl->nel",
        key_as_float * final_decay_weight[:, :, None],
        value_as_float,
        precision=highest_precision,
    )
    block_decay = jnp.where(jnp.all(continuation_flags), jnp.exp(cumulative_decay[-1]), 0.0)

    assert heads_here == 1
    chunk = key_width * value_width // group_count
    extras = block_decay
    extra_width = 128 * pl_cdiv(extras.shape[0], 128)
    extras = jnp.pad(extras, (0, extra_width - extras.shape[0]))
    payload = jnp.concatenate(
        [
            block_total_sum.reshape(group_count, chunk),
            jnp.broadcast_to(extras[None, :], (group_count, extra_width)),
        ],
        axis=1,
    )
    received = lax.all_to_all(payload, ("ga", "gb"), 0, 0, tiled=True)
    slices_in = received[:, :chunk]
    decay_all = received[:, chunk]
    blk = jnp.arange(group_count, dtype=jnp.int32)
    between = (blk[None, None, :] > blk[None, :, None]) & (blk[None, None, :] < blk[:, None, None])
    weights = jnp.prod(jnp.where(between, decay_all[None, None, :], 1.0), axis=2)
    weights = jnp.where(blk[None, :] < blk[:, None], weights, 0.0)
    slices_out = jnp.dot(weights, slices_in, precision=highest_precision)
    carried_state = lax.all_to_all(slices_out, ("ga", "gb"), 0, 0, tiled=True).reshape(
        heads_here, key_width, value_width
    )

    vocab_rows = lax.all_gather(vocab_weight, "ga", axis=0, tiled=True)
    vocab_rows, carried_state = lax.optimization_barrier((vocab_rows, carried_state))
    query_as_float = query_heads.astype(jnp.float32)
    state_contribution = (
        jnp.einsum("ugo,gow->ugw", query_as_float, carried_state, precision=highest_precision)
        * key_scaling
        * (jnp.exp(cumulative_decay) * continuation_flags[:, None].astype(jnp.float32))[:, :, None]
    )
    retained = in_block + state_contribution
    state_norms = jnp.log(
        1.0 + jnp.sqrt(jnp.mean(carried_state * carried_state, axis=(1, 2)) + 1e-06)
    )[None, :]
    normed = layer_norm(retained, 1e-06)
    gate_float = gate_proj.reshape(tok_count, heads_here, value_width).astype(jnp.float32)
    gated_out = (
        (normed * jax.nn.silu(gate_float))
        .astype(jnp.bfloat16)
        .reshape(tok_count, heads_here * value_width)
    )
    own_branch = lax.psum_scatter(
        jnp.dot(gated_out, out_weight, preferred_element_type=jnp.float32),
        "head",
        scatter_dimension=0,
        tiled=True,
    )
    stream = residual[0].astype(jnp.float32) + own_branch
    hidden = (layer_norm(stream, 1e-05) * norm_gain).astype(jnp.bfloat16)

    sub = lax.axis_size("gb")
    ga_index = lax.axis_index("ga")
    gb_index = lax.axis_index("gb")
    code = jnp.concatenate([targets[0] // 256, targets[0] % 256]).astype(jnp.bfloat16)
    code_row = jnp.pad(code, (0, hidden.shape[1] - code.shape[0]))[None, :]
    hidden_ext = jnp.concatenate([hidden, code_row], axis=0)
    gathered = lax.all_gather(lax.all_gather(hidden_ext, "head"), "gb")
    hidden_all = gathered[:, :, :slice_rows, :].reshape(-1, hidden.shape[1])
    code_all = gathered[:, :, slice_rows, : 2 * slice_rows].astype(jnp.int32)
    all_targets = (code_all[..., :slice_rows] * 256 + code_all[..., slice_rows:]).reshape(-1)
    part_count = lax.axis_size("ga")
    entry_ids = (
        (
            head_index * group_count
            + jnp.arange(part_count, dtype=jnp.int32)[:, None] * sub
            + gb_index
        )
        * vocab_here
        + jnp.arange(vocab_here, dtype=jnp.int32)[None, :]
    ).reshape(-1)
    logits = lax.dot_general(
        hidden_all,
        vocab_rows,
        (((1,), (1,)), ((), ())),
        preferred_element_type=jnp.float32,
    )
    top = jnp.max(logits, axis=1)
    exp_total = jnp.sum(jnp.exp(logits - top[:, None]), axis=1)
    picked = jnp.sum(jnp.where(entry_ids[None, :] == all_targets[:, None], logits, 0.0), axis=1)
    outgoing = jnp.stack([top, exp_total, picked]).reshape(3, sub, head_count, slice_rows)
    outgoing = jnp.transpose(outgoing, (2, 1, 0, 3)).reshape(head_count * sub, 3 * slice_rows)
    incoming = lax.all_to_all(outgoing, ("head", "gb"), 0, 0, tiled=True).reshape(
        head_count * sub, 3, slice_rows
    )
    own_max = jnp.max(incoming[:, 0], axis=0)
    own_total = jnp.sum(incoming[:, 1] * jnp.exp(incoming[:, 0] - own_max[None, :]), axis=0)
    own_target = jnp.sum(incoming[:, 2], axis=0)
    token_logp = own_target - own_max - jnp.log(own_total)
    token_ratio = response_mask[0].astype(jnp.float32) * (token_logp - ref_logp[0])
    own_positions = positions[0] + head_index * slice_rows + jnp.arange(slice_rows, dtype=jnp.int32)
    own_seq = jnp.sum((own_positions[:, None] >= starts[None, 1:]).astype(jnp.int32), axis=1)
    member = (own_seq[:, None] == jnp.arange(seq_count, dtype=jnp.int32)[None, :]).astype(
        jnp.float32
    )
    partial_sums = jnp.sum(member * token_ratio[:, None], axis=0)
    seq_total = partial_sums
    for axes in (("head", "gb"), "ga"):
        width = lax.axis_size(axes)
        spread = jnp.broadcast_to(seq_total[None, :], (width, seq_count))
        seq_total = jnp.sum(lax.all_to_all(spread, axes, 0, 0, tiled=True), axis=0)
    seq_ratio = seq_total / seq_lengths.astype(jnp.float32)
    return (seq_ratio, state_norms, own_max[None, :])


def pl_cdiv(a, b):
    return (a + b - 1) // b


def solution(mesh):
    from jax.sharding import Mesh

    head_size, group_size = mesh.devices.shape
    sub = 8 if group_size % 8 == 0 else 1
    fine = Mesh(
        mesh.devices.reshape(head_size, group_size // sub, sub), ("head", "ga", "gb")
    )
    group = ("ga", "gb")
    placed = (
        P(group, "head"),
        P(group, "head"),
        P(group, "head"),
        P(group, "head"),
        P(group, "head"),
        P("head", None),
        P(group, "head", None),
        P(),
        P(("head", "ga", "gb"), None),
        P(group, "head"),
        P(group, "head"),
        P(group, "head"),
        P(),
    )
    return jax.shard_map(
        per_device,
        mesh=fine,
        in_specs=placed,
        out_specs=(P(), P(group, "head"), P(group, "head")),
        check_vma=False,
    )
```

```python
import jax
import jax.numpy as jnp
from jax import lax
from jax.sharding import PartitionSpec as P


def layer_norm(stream, width_eps):
    mean_val = jnp.mean(stream, axis=-1, keepdims=True)
    centered = stream - mean_val
    var_val = jnp.mean(centered * centered, axis=-1, keepdims=True)
    return centered / jnp.sqrt(var_val + width_eps)


def per_device(
    query_proj,
    key_proj,
    value_proj,
    gate_proj,
    log_decay,
    out_weight,
    residual,
    norm_gain,
    vocab_weight,
    targets,
    ref_logp,
    response_mask,
    seq_lengths,
):
    highest_precision = lax.Precision.HIGHEST
    head_count = lax.axis_size("head")
    group_count = lax.axis_size(("ga", "gb"))
    head_index = lax.axis_index("head")
    group_index = lax.axis_index(("ga", "gb"))
    tok_count = query_proj.shape[0]
    heads_here = log_decay.shape[1]
    key_width = query_proj.shape[1] // heads_here
    value_width = value_proj.shape[1] // heads_here
    slice_rows = residual.shape[1]
    seq_count = seq_lengths.shape[0]
    vocab_here = vocab_weight.shape[0]
    key_scaling = key_width ** (-0.5)
    starts = jnp.cumsum(seq_lengths) - seq_lengths
    local_pos = jnp.arange(tok_count, dtype=jnp.int32)
    positions = group_index * tok_count + local_pos
    seq_ids = jnp.sum((positions[:, None] >= starts[None, 1:]).astype(jnp.int32), axis=1)
    is_start = jnp.any(positions[:, None] == starts[None, :], axis=1)
    cumulative_decay = jnp.cumsum(log_decay, axis=0)
    same_seq = (seq_ids[:, None] == seq_ids[None, :]) & (local_pos[None, :] <= local_pos[:, None])
    gap_log = cumulative_decay[:, None, :] - cumulative_decay[None, :, :]
    decay_mat = jnp.where(same_seq[:, :, None], jnp.exp(jnp.minimum(gap_log, 0.0)), 0.0)
    query_heads = query_proj.reshape(tok_count, heads_here, key_width)
    key_heads = key_proj.reshape(tok_count, heads_here, key_width)
    value_heads = value_proj.reshape(tok_count, heads_here, value_width)
    raw_scores = jnp.einsum(
        "thd,shd->tsh", query_heads, key_heads, preferred_element_type=jnp.float32
    )
    weights_in = (raw_scores * key_scaling * decay_mat).astype(jnp.bfloat16)
    in_block = jnp.einsum(
        "tsh,shv->thv", weights_in, value_heads, preferred_element_type=jnp.float32
    )
    continuation_flags = (seq_ids == seq_ids[0]) & jnp.logical_not(is_start[0])
    final_decay_weight = jnp.where(
        (seq_ids == seq_ids[-1])[:, None],
        jnp.exp(cumulative_decay[-1][None, :] - cumulative_decay),
        0.0,
    )
    key_as_float = key_heads.astype(jnp.float32)
    value_as_float = value_heads.astype(jnp.float32)
    block_total_sum = jnp.einsum(
        "ane,anl->nel",
        key_as_float * final_decay_weight[:, :, None],
        value_as_float,
        precision=highest_precision,
    )
    block_decay = jnp.where(jnp.all(continuation_flags), jnp.exp(cumulative_decay[-1]), 0.0)

    assert heads_here == 1
    chunk = key_width * value_width // group_count
    extras = block_decay
    extra_width = 128 * pl_cdiv(extras.shape[0], 128)
    extras = jnp.pad(extras, (0, extra_width - extras.shape[0]))
    payload = jnp.concatenate(
        [
            block_total_sum.reshape(group_count, chunk),
            jnp.broadcast_to(extras[None, :], (group_count, extra_width)),
        ],
        axis=1,
    )
    received = lax.all_to_all(payload, ("ga", "gb"), 0, 0, tiled=True)
    slices_in = received[:, :chunk]
    decay_all = received[:, chunk]
    blk = jnp.arange(group_count, dtype=jnp.int32)
    between = (blk[None, None, :] > blk[None, :, None]) & (blk[None, None, :] < blk[:, None, None])
    weights = jnp.prod(jnp.where(between, decay_all[None, None, :], 1.0), axis=2)
    weights = jnp.where(blk[None, :] < blk[:, None], weights, 0.0)
    slices_out = jnp.dot(weights, slices_in, precision=highest_precision)
    carried_state = lax.all_to_all(slices_out, ("ga", "gb"), 0, 0, tiled=True).reshape(
        heads_here, key_width, value_width
    )

    vocab_rows = lax.all_gather(vocab_weight, "ga", axis=0, tiled=True)
    vocab_rows, carried_state = lax.optimization_barrier((vocab_rows, carried_state))
    query_as_float = query_heads.astype(jnp.float32)
    state_contribution = (
        jnp.einsum("ugo,gow->ugw", query_as_float, carried_state, precision=highest_precision)
        * key_scaling
        * (jnp.exp(cumulative_decay) * continuation_flags[:, None].astype(jnp.float32))[:, :, None]
    )
    retained = in_block + state_contribution
    state_norms = jnp.log(
        1.0 + jnp.sqrt(jnp.mean(carried_state * carried_state, axis=(1, 2)) + 1e-06)
    )[None, :]
    normed = layer_norm(retained, 1e-06)
    gate_float = gate_proj.reshape(tok_count, heads_here, value_width).astype(jnp.float32)
    gated_out = (
        (normed * jax.nn.silu(gate_float))
        .astype(jnp.bfloat16)
        .reshape(tok_count, heads_here * value_width)
    )
    own_branch = lax.psum_scatter(
        jnp.dot(gated_out, out_weight, preferred_element_type=jnp.float32),
        "head",
        scatter_dimension=0,
        tiled=True,
    )
    stream = residual[0].astype(jnp.float32) + own_branch
    hidden = (layer_norm(stream, 1e-05) * norm_gain).astype(jnp.bfloat16)

    sub = lax.axis_size("gb")
    ga_index = lax.axis_index("ga")
    gb_index = lax.axis_index("gb")
    code = jnp.concatenate([targets[0] // 256, targets[0] % 256]).astype(jnp.bfloat16)
    code_row = jnp.pad(code, (0, hidden.shape[1] - code.shape[0]))[None, :]
    hidden_ext = jnp.concatenate([hidden, code_row], axis=0)
    gathered = lax.all_gather(lax.all_gather(hidden_ext, "head"), "gb")
    code_all = gathered[:, :, slice_rows, : 2 * slice_rows].astype(jnp.int32)
    all_targets = (code_all[..., :slice_rows] * 256 + code_all[..., slice_rows:]).reshape(-1)
    part_count = lax.axis_size("ga")
    entry_ids = (
        (
            head_index * group_count
            + jnp.arange(part_count, dtype=jnp.int32)[:, None] * sub
            + gb_index
        )
        * vocab_here
        + jnp.arange(vocab_here, dtype=jnp.int32)[None, :]
    ).reshape(-1)
    logits = lax.dot_general(
        gathered.reshape(-1, hidden.shape[1]),
        vocab_rows,
        (((1,), (1,)), ((), ())),
        preferred_element_type=jnp.float32,
    ).reshape(head_count * sub, slice_rows + 1, -1)[:, :slice_rows, :].reshape(
        head_count * sub * slice_rows, -1
    )
    top = jnp.max(logits, axis=1)
    exp_total = jnp.sum(jnp.exp(logits - top[:, None]), axis=1)
    picked = jnp.sum(jnp.where(entry_ids[None, :] == all_targets[:, None], logits, 0.0), axis=1)
    outgoing = jnp.stack([top, exp_total, picked]).reshape(3, sub, head_count, slice_rows)
    outgoing = jnp.transpose(outgoing, (2, 1, 0, 3)).reshape(head_count * sub, 3 * slice_rows)
    incoming = lax.all_to_all(outgoing, ("head", "gb"), 0, 0, tiled=True).reshape(
        head_count * sub, 3, slice_rows
    )
    own_max = jnp.max(incoming[:, 0], axis=0)
    own_total = jnp.sum(incoming[:, 1] * jnp.exp(incoming[:, 0] - own_max[None, :]), axis=0)
    own_target = jnp.sum(incoming[:, 2], axis=0)
    token_logp = own_target - own_max - jnp.log(own_total)
    token_ratio = response_mask[0].astype(jnp.float32) * (token_logp - ref_logp[0])
    own_positions = positions[0] + head_index * slice_rows + jnp.arange(slice_rows, dtype=jnp.int32)
    own_seq = jnp.sum((own_positions[:, None] >= starts[None, 1:]).astype(jnp.int32), axis=1)
    member = (own_seq[:, None] == jnp.arange(seq_count, dtype=jnp.int32)[None, :]).astype(
        jnp.float32
    )
    partial_sums = jnp.sum(member * token_ratio[:, None], axis=0)
    seq_total = partial_sums
    for axes in (("head", "gb"), "ga"):
        width = lax.axis_size(axes)
        spread = jnp.broadcast_to(seq_total[None, :], (width, seq_count))
        seq_total = jnp.sum(lax.all_to_all(spread, axes, 0, 0, tiled=True), axis=0)
    seq_ratio = seq_total / seq_lengths.astype(jnp.float32)
    return (seq_ratio, state_norms, own_max[None, :])


def pl_cdiv(a, b):
    return (a + b - 1) // b


def solution(mesh):
    from jax.sharding import Mesh

    head_size, group_size = mesh.devices.shape
    sub = 8 if group_size % 8 == 0 else 1
    fine = Mesh(
        mesh.devices.reshape(head_size, group_size // sub, sub), ("head", "ga", "gb")
    )
    group = ("ga", "gb")
    placed = (
        P(group, "head"),
        P(group, "head"),
        P(group, "head"),
        P(group, "head"),
        P(group, "head"),
        P("head", None),
        P(group, "head", None),
        P(),
        P(("head", "ga", "gb"), None),
        P(group, "head"),
        P(group, "head"),
        P(group, "head"),
        P(),
    )
    return jax.shard_map(
        per_device,
        mesh=fine,
        in_specs=placed,
        out_specs=(P(), P(group, "head"), P(group, "head")),
        check_vma=False,
    )
```

```python
import jax
import jax.numpy as jnp
from jax import lax
from jax.sharding import PartitionSpec as P


def layer_norm(stream, width_eps):
    mean_val = jnp.mean(stream, axis=-1, keepdims=True)
    centered = stream - mean_val
    var_val = jnp.mean(centered * centered, axis=-1, keepdims=True)
    return centered / jnp.sqrt(var_val + width_eps)


def per_device(
    query_proj,
    key_proj,
    value_proj,
    gate_proj,
    log_decay,
    out_weight,
    residual,
    norm_gain,
    vocab_weight,
    targets,
    ref_logp,
    response_mask,
    seq_lengths,
):
    highest_precision = lax.Precision.HIGHEST
    head_count = lax.axis_size("head")
    group_count = lax.axis_size(("ga", "gb"))
    head_index = lax.axis_index("head")
    group_index = lax.axis_index(("ga", "gb"))
    tok_count = query_proj.shape[0]
    heads_here = log_decay.shape[1]
    key_width = query_proj.shape[1] // heads_here
    value_width = value_proj.shape[1] // heads_here
    slice_rows = residual.shape[1]
    seq_count = seq_lengths.shape[0]
    vocab_here = vocab_weight.shape[0]
    key_scaling = key_width ** (-0.5)
    starts = jnp.cumsum(seq_lengths) - seq_lengths
    local_pos = jnp.arange(tok_count, dtype=jnp.int32)
    positions = group_index * tok_count + local_pos
    seq_ids = jnp.sum((positions[:, None] >= starts[None, 1:]).astype(jnp.int32), axis=1)
    is_start = jnp.any(positions[:, None] == starts[None, :], axis=1)
    cumulative_decay = jnp.cumsum(log_decay, axis=0)
    same_seq = (seq_ids[:, None] == seq_ids[None, :]) & (local_pos[None, :] <= local_pos[:, None])
    gap_log = cumulative_decay[:, None, :] - cumulative_decay[None, :, :]
    decay_mat = jnp.where(same_seq[:, :, None], jnp.exp(jnp.minimum(gap_log, 0.0)), 0.0)
    query_heads = query_proj.reshape(tok_count, heads_here, key_width)
    key_heads = key_proj.reshape(tok_count, heads_here, key_width)
    value_heads = value_proj.reshape(tok_count, heads_here, value_width)
    raw_scores = jnp.einsum(
        "thd,shd->tsh", query_heads, key_heads, preferred_element_type=jnp.float32
    )
    weights_in = (raw_scores * key_scaling * decay_mat).astype(jnp.bfloat16)
    in_block = jnp.einsum(
        "tsh,shv->thv", weights_in, value_heads, preferred_element_type=jnp.float32
    )
    continuation_flags = (seq_ids == seq_ids[0]) & jnp.logical_not(is_start[0])
    final_decay_weight = jnp.where(
        (seq_ids == seq_ids[-1])[:, None],
        jnp.exp(cumulative_decay[-1][None, :] - cumulative_decay),
        0.0,
    )
    key_as_float = key_heads.astype(jnp.float32)
    value_as_float = value_heads.astype(jnp.float32)
    block_total_sum = jnp.einsum(
        "ane,anl->nel",
        key_as_float * final_decay_weight[:, :, None],
        value_as_float,
        precision=highest_precision,
    )
    block_decay = jnp.where(jnp.all(continuation_flags), jnp.exp(cumulative_decay[-1]), 0.0)

    assert heads_here == 1
    chunk = key_width * value_width // group_count
    extras = block_decay
    extra_width = 128 * pl_cdiv(extras.shape[0], 128)
    extras = jnp.pad(extras, (0, extra_width - extras.shape[0]))
    payload = jnp.concatenate(
        [
            block_total_sum.reshape(group_count, chunk),
            jnp.broadcast_to(extras[None, :], (group_count, extra_width)),
        ],
        axis=1,
    )
    received = lax.all_to_all(payload, ("ga", "gb"), 0, 0, tiled=True)
    slices_in = received[:, :chunk]
    decay_all = received[:, chunk]
    blk = jnp.arange(group_count, dtype=jnp.int32)
    between = (blk[None, None, :] > blk[None, :, None]) & (blk[None, None, :] < blk[:, None, None])
    weights = jnp.prod(jnp.where(between, decay_all[None, None, :], 1.0), axis=2)
    weights = jnp.where(blk[None, :] < blk[:, None], weights, 0.0)
    slices_out = jnp.dot(weights, slices_in, precision=highest_precision)
    carried_state = lax.all_to_all(slices_out, ("ga", "gb"), 0, 0, tiled=True).reshape(
        heads_here, key_width, value_width
    )

    vocab_rows = lax.all_gather(vocab_weight, "ga", axis=0, tiled=True)
    vocab_rows, carried_state = lax.optimization_barrier((vocab_rows, carried_state))
    query_as_float = query_heads.astype(jnp.float32)
    state_contribution = (
        jnp.einsum("ugo,gow->ugw", query_as_float, carried_state, precision=highest_precision)
        * key_scaling
        * (jnp.exp(cumulative_decay) * continuation_flags[:, None].astype(jnp.float32))[:, :, None]
    )
    retained = in_block + state_contribution
    state_norms = jnp.log(
        1.0 + jnp.sqrt(jnp.mean(carried_state * carried_state, axis=(1, 2)) + 1e-06)
    )[None, :]
    normed = layer_norm(retained, 1e-06)
    gate_float = gate_proj.reshape(tok_count, heads_here, value_width).astype(jnp.float32)
    gated_out = (
        (normed * jax.nn.silu(gate_float))
        .astype(jnp.bfloat16)
        .reshape(tok_count, heads_here * value_width)
    )
    branch_parts = jnp.dot(gated_out, out_weight, preferred_element_type=jnp.float32)
    own_branch = jnp.sum(
        lax.all_to_all(
            branch_parts.reshape(head_count, slice_rows, -1), "head", 0, 0, tiled=True
        ),
        axis=0,
    )
    stream = residual[0].astype(jnp.float32) + own_branch
    hidden = (layer_norm(stream, 1e-05) * norm_gain).astype(jnp.bfloat16)

    sub = lax.axis_size("gb")
    ga_index = lax.axis_index("ga")
    gb_index = lax.axis_index("gb")
    code = jnp.concatenate([targets[0] // 256, targets[0] % 256]).astype(jnp.bfloat16)
    code_row = jnp.pad(code, (0, hidden.shape[1] - code.shape[0]))[None, :]
    hidden_ext = jnp.concatenate([hidden, code_row], axis=0)
    gathered = lax.all_gather(lax.all_gather(hidden_ext, "head"), "gb")
    code_all = gathered[:, :, slice_rows, : 2 * slice_rows].astype(jnp.int32)
    all_targets = (code_all[..., :slice_rows] * 256 + code_all[..., slice_rows:]).reshape(-1)
    part_count = lax.axis_size("ga")
    entry_ids = (
        (
            head_index * group_count
            + jnp.arange(part_count, dtype=jnp.int32)[:, None] * sub
            + gb_index
        )
        * vocab_here
        + jnp.arange(vocab_here, dtype=jnp.int32)[None, :]
    ).reshape(-1)
    logits = lax.dot_general(
        gathered.reshape(-1, hidden.shape[1]),
        vocab_rows,
        (((1,), (1,)), ((), ())),
        preferred_element_type=jnp.float32,
    ).reshape(head_count * sub, slice_rows + 1, -1)[:, :slice_rows, :].reshape(
        head_count * sub * slice_rows, -1
    )
    top = jnp.max(logits, axis=1)
    exp_total = jnp.sum(jnp.exp(logits - top[:, None]), axis=1)
    picked = jnp.sum(jnp.where(entry_ids[None, :] == all_targets[:, None], logits, 0.0), axis=1)
    outgoing = jnp.stack([top, exp_total, picked]).reshape(3, sub, head_count, slice_rows)
    outgoing = jnp.transpose(outgoing, (2, 1, 0, 3)).reshape(head_count * sub, 3 * slice_rows)
    incoming = lax.all_to_all(outgoing, ("head", "gb"), 0, 0, tiled=True).reshape(
        head_count * sub, 3, slice_rows
    )
    own_max = jnp.max(incoming[:, 0], axis=0)
    own_total = jnp.sum(incoming[:, 1] * jnp.exp(incoming[:, 0] - own_max[None, :]), axis=0)
    own_target = jnp.sum(incoming[:, 2], axis=0)
    token_logp = own_target - own_max - jnp.log(own_total)
    token_ratio = response_mask[0].astype(jnp.float32) * (token_logp - ref_logp[0])
    own_positions = positions[0] + head_index * slice_rows + jnp.arange(slice_rows, dtype=jnp.int32)
    own_seq = jnp.sum((own_positions[:, None] >= starts[None, 1:]).astype(jnp.int32), axis=1)
    member = (own_seq[:, None] == jnp.arange(seq_count, dtype=jnp.int32)[None, :]).astype(
        jnp.float32
    )
    partial_sums = jnp.sum(member * token_ratio[:, None], axis=0)
    seq_total = partial_sums
    for axes in (("head", "gb"), "ga"):
        width = lax.axis_size(axes)
        spread = jnp.broadcast_to(seq_total[None, :], (width, seq_count))
        seq_total = jnp.sum(lax.all_to_all(spread, axes, 0, 0, tiled=True), axis=0)
    seq_ratio = seq_total / seq_lengths.astype(jnp.float32)
    return (seq_ratio, state_norms, own_max[None, :])


def pl_cdiv(a, b):
    return (a + b - 1) // b


def solution(mesh):
    from jax.sharding import Mesh

    head_size, group_size = mesh.devices.shape
    sub = 8 if group_size % 8 == 0 else 1
    fine = Mesh(
        mesh.devices.reshape(head_size, group_size // sub, sub), ("head", "ga", "gb")
    )
    group = ("ga", "gb")
    placed = (
        P(group, "head"),
        P(group, "head"),
        P(group, "head"),
        P(group, "head"),
        P(group, "head"),
        P("head", None),
        P(group, "head", None),
        P(),
        P(("head", "ga", "gb"), None),
        P(group, "head"),
        P(group, "head"),
        P(group, "head"),
        P(),
    )
    return jax.shard_map(
        per_device,
        mesh=fine,
        in_specs=placed,
        out_specs=(P(), P(group, "head"), P(group, "head")),
        check_vma=False,
    )
```

```python
import jax
import jax.numpy as jnp
from jax import lax
from jax.sharding import PartitionSpec as P


def layer_norm(stream, width_eps):
    mean_val = jnp.mean(stream, axis=-1, keepdims=True)
    centered = stream - mean_val
    var_val = jnp.mean(centered * centered, axis=-1, keepdims=True)
    return centered / jnp.sqrt(var_val + width_eps)


def per_device(
    query_proj,
    key_proj,
    value_proj,
    gate_proj,
    log_decay,
    out_weight,
    residual,
    norm_gain,
    vocab_weight,
    targets,
    ref_logp,
    response_mask,
    seq_lengths,
):
    highest_precision = lax.Precision.HIGHEST
    head_count = lax.axis_size("head")
    group_count = lax.axis_size(("ga", "gb"))
    head_index = lax.axis_index("head")
    group_index = lax.axis_index(("ga", "gb"))
    tok_count = query_proj.shape[0]
    heads_here = log_decay.shape[1]
    key_width = query_proj.shape[1] // heads_here
    value_width = value_proj.shape[1] // heads_here
    slice_rows = residual.shape[1]
    seq_count = seq_lengths.shape[0]
    vocab_here = vocab_weight.shape[0]
    key_scaling = key_width ** (-0.5)
    starts = jnp.cumsum(seq_lengths) - seq_lengths
    local_pos = jnp.arange(tok_count, dtype=jnp.int32)
    positions = group_index * tok_count + local_pos
    seq_ids = jnp.sum((positions[:, None] >= starts[None, 1:]).astype(jnp.int32), axis=1)
    is_start = jnp.any(positions[:, None] == starts[None, :], axis=1)
    cumulative_decay = jnp.cumsum(log_decay, axis=0)
    same_seq = (seq_ids[:, None] == seq_ids[None, :]) & (local_pos[None, :] <= local_pos[:, None])
    gap_log = cumulative_decay[:, None, :] - cumulative_decay[None, :, :]
    decay_mat = jnp.where(same_seq[:, :, None], jnp.exp(jnp.minimum(gap_log, 0.0)), 0.0)
    query_heads = query_proj.reshape(tok_count, heads_here, key_width)
    key_heads = key_proj.reshape(tok_count, heads_here, key_width)
    value_heads = value_proj.reshape(tok_count, heads_here, value_width)
    raw_scores = jnp.einsum(
        "thd,shd->tsh", query_heads, key_heads, preferred_element_type=jnp.float32
    )
    weights_in = (raw_scores * key_scaling * decay_mat).astype(jnp.bfloat16)
    in_block = jnp.einsum(
        "tsh,shv->thv", weights_in, value_heads, preferred_element_type=jnp.float32
    )
    continuation_flags = (seq_ids == seq_ids[0]) & jnp.logical_not(is_start[0])
    final_decay_weight = jnp.where(
        (seq_ids == seq_ids[-1])[:, None],
        jnp.exp(cumulative_decay[-1][None, :] - cumulative_decay),
        0.0,
    )
    key_as_float = key_heads.astype(jnp.float32)
    value_as_float = value_heads.astype(jnp.float32)
    block_total_sum = jnp.einsum(
        "ane,anl->nel",
        key_as_float * final_decay_weight[:, :, None],
        value_as_float,
        precision=highest_precision,
    )
    block_decay = jnp.where(jnp.all(continuation_flags), jnp.exp(cumulative_decay[-1]), 0.0)

    assert heads_here == 1
    chunk = key_width * value_width // group_count
    extras = block_decay
    extra_width = 128 * pl_cdiv(extras.shape[0], 128)
    extras = jnp.pad(extras, (0, extra_width - extras.shape[0]))
    payload = jnp.concatenate(
        [
            block_total_sum.reshape(group_count, chunk),
            jnp.broadcast_to(extras[None, :], (group_count, extra_width)),
        ],
        axis=1,
    )
    received = lax.all_to_all(payload, ("ga", "gb"), 0, 0, tiled=True)
    slices_in = received[:, :chunk]
    decay_all = received[:, chunk]
    blk = jnp.arange(group_count, dtype=jnp.int32)
    between = (blk[None, None, :] > blk[None, :, None]) & (blk[None, None, :] < blk[:, None, None])
    weights = jnp.prod(jnp.where(between, decay_all[None, None, :], 1.0), axis=2)
    weights = jnp.where(blk[None, :] < blk[:, None], weights, 0.0)
    slices_out = jnp.dot(weights, slices_in, precision=highest_precision)
    carried_state = lax.all_to_all(slices_out, ("ga", "gb"), 0, 0, tiled=True).reshape(
        heads_here, key_width, value_width
    )

    vocab_rows = lax.all_gather(vocab_weight, "ga", axis=0, tiled=True)
    vocab_rows, carried_state = lax.optimization_barrier((vocab_rows, carried_state))
    query_as_float = query_heads.astype(jnp.float32)
    state_contribution = (
        jnp.einsum("ugo,gow->ugw", query_as_float, carried_state, precision=highest_precision)
        * key_scaling
        * (jnp.exp(cumulative_decay) * continuation_flags[:, None].astype(jnp.float32))[:, :, None]
    )
    retained = in_block + state_contribution
    state_norms = jnp.log(
        1.0 + jnp.sqrt(jnp.mean(carried_state * carried_state, axis=(1, 2)) + 1e-06)
    )[None, :]
    normed = layer_norm(retained, 1e-06)
    gate_float = gate_proj.reshape(tok_count, heads_here, value_width).astype(jnp.float32)
    gated_out = (
        (normed * jax.nn.silu(gate_float))
        .astype(jnp.bfloat16)
        .reshape(tok_count, heads_here * value_width)
    )
    branch_parts = jnp.dot(gated_out, out_weight, preferred_element_type=jnp.float32)
    own_branch = jnp.sum(
        lax.all_to_all(
            branch_parts.reshape(head_count, slice_rows, -1), "head", 0, 0, tiled=True
        ),
        axis=0,
    )
    stream = residual[0].astype(jnp.float32) + own_branch
    hidden = (layer_norm(stream, 1e-05) * norm_gain).astype(jnp.bfloat16)

    sub = lax.axis_size("gb")
    ga_index = lax.axis_index("ga")
    gb_index = lax.axis_index("gb")
    code = jnp.concatenate([targets[0] // 256, targets[0] % 256]).astype(jnp.bfloat16)
    code_row = jnp.pad(code, (0, hidden.shape[1] - code.shape[0]))[None, :]
    hidden_ext = jnp.concatenate([hidden, code_row], axis=0)
    gathered = lax.all_gather(lax.all_gather(hidden_ext, "head"), "gb")
    code_all = gathered[:, :, slice_rows, : 2 * slice_rows].astype(jnp.int32)
    all_targets = (code_all[..., :slice_rows] * 256 + code_all[..., slice_rows:]).reshape(-1)
    part_count = lax.axis_size("ga")
    entry_ids = (
        (
            head_index * group_count
            + jnp.arange(part_count, dtype=jnp.int32)[:, None] * sub
            + gb_index
        )
        * vocab_here
        + jnp.arange(vocab_here, dtype=jnp.int32)[None, :]
    ).reshape(-1)
    logits = lax.dot_general(
        gathered.reshape(-1, hidden.shape[1]),
        vocab_rows,
        (((1,), (1,)), ((), ())),
        preferred_element_type=jnp.float32,
    ).reshape(head_count * sub, slice_rows + 1, -1)[:, :slice_rows, :].reshape(
        head_count * sub * slice_rows, -1
    )
    top = jnp.max(logits, axis=1)
    exp_total = jnp.sum(jnp.exp(logits - top[:, None]), axis=1)
    picked = jnp.sum(jnp.where(entry_ids[None, :] == all_targets[:, None], logits, 0.0), axis=1)
    outgoing = jnp.stack([top, exp_total, picked]).reshape(3, sub, head_count, slice_rows)
    outgoing = jnp.transpose(outgoing, (2, 1, 0, 3)).reshape(head_count * sub, 3 * slice_rows)
    incoming = lax.all_to_all(outgoing, ("head", "gb"), 0, 0, tiled=True).reshape(
        head_count * sub, 3, slice_rows
    )
    own_max = jnp.max(incoming[:, 0], axis=0)
    own_total = jnp.sum(incoming[:, 1] * jnp.exp(incoming[:, 0] - own_max[None, :]), axis=0)
    own_target = jnp.sum(incoming[:, 2], axis=0)
    token_logp = own_target - own_max - jnp.log(own_total)
    token_ratio = response_mask[0].astype(jnp.float32) * (token_logp - ref_logp[0])
    own_positions = positions[0] + head_index * slice_rows + jnp.arange(slice_rows, dtype=jnp.int32)
    own_seq = jnp.sum((own_positions[:, None] >= starts[None, 1:]).astype(jnp.int32), axis=1)
    member = (own_seq[:, None] == jnp.arange(seq_count, dtype=jnp.int32)[None, :]).astype(
        jnp.float32
    )
    partial_sums = jnp.sum(member * token_ratio[:, None], axis=0)
    seq_total = partial_sums
    for axes in (("head", "ga", "gb"),):
        width = lax.axis_size(axes)
        spread = jnp.broadcast_to(seq_total[None, :], (width, seq_count))
        seq_total = jnp.sum(lax.all_to_all(spread, axes, 0, 0, tiled=True), axis=0)
    seq_ratio = seq_total / seq_lengths.astype(jnp.float32)
    return (seq_ratio, state_norms, own_max[None, :])


def pl_cdiv(a, b):
    return (a + b - 1) // b


def solution(mesh):
    from jax.sharding import Mesh

    head_size, group_size = mesh.devices.shape
    sub = 8 if group_size % 8 == 0 else 1
    fine = Mesh(
        mesh.devices.reshape(head_size, group_size // sub, sub), ("head", "ga", "gb")
    )
    group = ("ga", "gb")
    placed = (
        P(group, "head"),
        P(group, "head"),
        P(group, "head"),
        P(group, "head"),
        P(group, "head"),
        P("head", None),
        P(group, "head", None),
        P(),
        P(("head", "ga", "gb"), None),
        P(group, "head"),
        P(group, "head"),
        P(group, "head"),
        P(),
    )
    return jax.shard_map(
        per_device,
        mesh=fine,
        in_specs=placed,
        out_specs=(P(), P(group, "head"), P(group, "head")),
        check_vma=False,
    )
```

```python
import jax
import jax.numpy as jnp
from jax import lax
from jax.sharding import PartitionSpec as P


def layer_norm(stream, width_eps):
    mean_val = jnp.mean(stream, axis=-1, keepdims=True)
    centered = stream - mean_val
    var_val = jnp.mean(centered * centered, axis=-1, keepdims=True)
    return centered / jnp.sqrt(var_val + width_eps)


def per_device(
    query_proj,
    key_proj,
    value_proj,
    gate_proj,
    log_decay,
    out_weight,
    residual,
    norm_gain,
    vocab_weight,
    targets,
    ref_logp,
    response_mask,
    seq_lengths,
):
    highest_precision = lax.Precision.HIGHEST
    head_count = lax.axis_size("head")
    group_count = lax.axis_size(("ga", "gb"))
    head_index = lax.axis_index("head")
    group_index = lax.axis_index(("ga", "gb"))
    tok_count = query_proj.shape[0]
    heads_here = log_decay.shape[1]
    key_width = query_proj.shape[1] // heads_here
    value_width = value_proj.shape[1] // heads_here
    slice_rows = residual.shape[1]
    seq_count = seq_lengths.shape[0]
    vocab_here = vocab_weight.shape[0]
    key_scaling = key_width ** (-0.5)
    starts = jnp.cumsum(seq_lengths) - seq_lengths
    local_pos = jnp.arange(tok_count, dtype=jnp.int32)
    positions = group_index * tok_count + local_pos
    seq_ids = jnp.sum((positions[:, None] >= starts[None, 1:]).astype(jnp.int32), axis=1)
    is_start = jnp.any(positions[:, None] == starts[None, :], axis=1)
    cumulative_decay = jnp.cumsum(log_decay, axis=0)
    same_seq = (seq_ids[:, None] == seq_ids[None, :]) & (local_pos[None, :] <= local_pos[:, None])
    gap_log = cumulative_decay[:, None, :] - cumulative_decay[None, :, :]
    decay_mat = jnp.where(same_seq[:, :, None], jnp.exp(jnp.minimum(gap_log, 0.0)), 0.0)
    query_heads = query_proj.reshape(tok_count, heads_here, key_width)
    key_heads = key_proj.reshape(tok_count, heads_here, key_width)
    value_heads = value_proj.reshape(tok_count, heads_here, value_width)
    raw_scores = jnp.einsum(
        "thd,shd->tsh", query_heads, key_heads, preferred_element_type=jnp.float32
    )
    weights_in = (raw_scores * key_scaling * decay_mat).astype(jnp.bfloat16)
    in_block = jnp.einsum(
        "tsh,shv->thv", weights_in, value_heads, preferred_element_type=jnp.float32
    )
    continuation_flags = (seq_ids == seq_ids[0]) & jnp.logical_not(is_start[0])
    final_decay_weight = jnp.where(
        (seq_ids == seq_ids[-1])[:, None],
        jnp.exp(cumulative_decay[-1][None, :] - cumulative_decay),
        0.0,
    )
    key_as_float = key_heads.astype(jnp.float32)
    value_as_float = value_heads.astype(jnp.float32)
    block_total_sum = jnp.einsum(
        "ane,anl->nel",
        key_as_float * final_decay_weight[:, :, None],
        value_as_float,
        precision=highest_precision,
    )
    block_decay = jnp.where(jnp.all(continuation_flags), jnp.exp(cumulative_decay[-1]), 0.0)

    assert heads_here == 1
    sub = lax.axis_size("gb")
    part_count = lax.axis_size("ga")
    state_size = key_width * value_width
    pad = jnp.zeros((127,), jnp.float32)
    chunk = state_size // sub
    extras = jnp.concatenate([block_decay, pad])
    payload = jnp.concatenate(
        [
            block_total_sum.reshape(sub, chunk),
            jnp.broadcast_to(extras[None, :], (sub, 128)),
        ],
        axis=1,
    )
    received = lax.all_to_all(payload, "gb", 0, 0, tiled=True)
    slices_in = received[:, :chunk]
    decay_in = received[:, chunk]
    local_in = jnp.dot(decay_weights(decay_in), slices_in, precision=highest_precision)
    tail_weights = decay_weights(jnp.concatenate([decay_in, jnp.ones((1,), jnp.float32)]))[
        sub, :sub
    ]
    octet_total = jnp.dot(tail_weights, slices_in, precision=highest_precision)
    octet_decay = jnp.prod(decay_in)
    lead_decay = jnp.cumprod(jnp.concatenate([jnp.ones((1,), jnp.float32), decay_in[:-1]]))
    piece = chunk // part_count
    extras = jnp.concatenate([octet_decay[None], pad])
    payload = jnp.concatenate(
        [
            octet_total.reshape(part_count, piece),
            jnp.broadcast_to(extras[None, :], (part_count, 128)),
        ],
        axis=1,
    )
    received = lax.all_to_all(payload, "ga", 0, 0, tiled=True)
    octet_in = jnp.dot(
        decay_weights(received[:, piece]), received[:, :piece], precision=highest_precision
    )
    octet_in = lax.all_to_all(octet_in, "ga", 0, 0, tiled=True).reshape(chunk)
    slices_out = local_in + lead_decay[:, None] * octet_in[None, :]
    carried_state = lax.all_to_all(slices_out, "gb", 0, 0, tiled=True).reshape(
        heads_here, key_width, value_width
    )

    vocab_rows = lax.all_gather(vocab_weight, "ga", axis=0, tiled=True)
    vocab_rows, carried_state = lax.optimization_barrier((vocab_rows, carried_state))
    query_as_float = query_heads.astype(jnp.float32)
    state_contribution = (
        jnp.einsum("ugo,gow->ugw", query_as_float, carried_state, precision=highest_precision)
        * key_scaling
        * (jnp.exp(cumulative_decay) * continuation_flags[:, None].astype(jnp.float32))[:, :, None]
    )
    retained = in_block + state_contribution
    state_norms = jnp.log(
        1.0 + jnp.sqrt(jnp.mean(carried_state * carried_state, axis=(1, 2)) + 1e-06)
    )[None, :]
    normed = layer_norm(retained, 1e-06)
    gate_float = gate_proj.reshape(tok_count, heads_here, value_width).astype(jnp.float32)
    gated_out = (
        (normed * jax.nn.silu(gate_float))
        .astype(jnp.bfloat16)
        .reshape(tok_count, heads_here * value_width)
    )
    branch_parts = jnp.dot(gated_out, out_weight, preferred_element_type=jnp.float32)
    own_branch = jnp.sum(
        lax.all_to_all(
            branch_parts.reshape(head_count, slice_rows, -1), "head", 0, 0, tiled=True
        ),
        axis=0,
    )
    stream = residual[0].astype(jnp.float32) + own_branch
    hidden = (layer_norm(stream, 1e-05) * norm_gain).astype(jnp.bfloat16)

    ga_index = lax.axis_index("ga")
    gb_index = lax.axis_index("gb")
    code = jnp.concatenate([targets[0] // 256, targets[0] % 256]).astype(jnp.bfloat16)
    code_row = jnp.pad(code, (0, hidden.shape[1] - code.shape[0]))[None, :]
    hidden_ext = jnp.concatenate([hidden, code_row], axis=0)
    gathered = lax.all_gather(lax.all_gather(hidden_ext, "head"), "gb")
    code_all = gathered[:, :, slice_rows, : 2 * slice_rows].astype(jnp.int32)
    all_targets = (code_all[..., :slice_rows] * 256 + code_all[..., slice_rows:]).reshape(-1)
    entry_ids = (
        (
            head_index * group_count
            + jnp.arange(part_count, dtype=jnp.int32)[:, None] * sub
            + gb_index
        )
        * vocab_here
        + jnp.arange(vocab_here, dtype=jnp.int32)[None, :]
    ).reshape(-1)
    logits = lax.dot_general(
        gathered.reshape(-1, hidden.shape[1]),
        vocab_rows,
        (((1,), (1,)), ((), ())),
        preferred_element_type=jnp.float32,
    ).reshape(head_count * sub, slice_rows + 1, -1)[:, :slice_rows, :].reshape(
        head_count * sub * slice_rows, -1
    )
    top = jnp.max(logits, axis=1)
    exp_total = jnp.sum(jnp.exp(logits - top[:, None]), axis=1)
    picked = jnp.sum(jnp.where(entry_ids[None, :] == all_targets[:, None], logits, 0.0), axis=1)
    outgoing = jnp.stack([top, exp_total, picked]).reshape(3, sub, head_count, slice_rows)
    outgoing = jnp.transpose(outgoing, (2, 1, 0, 3)).reshape(head_count * sub, 3 * slice_rows)
    incoming = lax.all_to_all(outgoing, ("head", "gb"), 0, 0, tiled=True).reshape(
        head_count * sub, 3, slice_rows
    )
    own_max = jnp.max(incoming[:, 0], axis=0)
    own_total = jnp.sum(incoming[:, 1] * jnp.exp(incoming[:, 0] - own_max[None, :]), axis=0)
    own_target = jnp.sum(incoming[:, 2], axis=0)
    token_logp = own_target - own_max - jnp.log(own_total)
    token_ratio = response_mask[0].astype(jnp.float32) * (token_logp - ref_logp[0])
    own_positions = positions[0] + head_index * slice_rows + jnp.arange(slice_rows, dtype=jnp.int32)
    own_seq = jnp.sum((own_positions[:, None] >= starts[None, 1:]).astype(jnp.int32), axis=1)
    member = (own_seq[:, None] == jnp.arange(seq_count, dtype=jnp.int32)[None, :]).astype(
        jnp.float32
    )
    partial_sums = jnp.sum(member * token_ratio[:, None], axis=0)
    seq_total = partial_sums
    for axes in (("head", "gb"), "ga"):
        width = lax.axis_size(axes)
        spread = jnp.broadcast_to(seq_total[None, :], (width, seq_count))
        seq_total = jnp.sum(lax.all_to_all(spread, axes, 0, 0, tiled=True), axis=0)
    seq_ratio = seq_total / seq_lengths.astype(jnp.float32)
    return (seq_ratio, state_norms, own_max[None, :])


def decay_weights(decay):
    count = decay.shape[0]
    at = jnp.arange(count, dtype=jnp.int32)
    between = (at[None, None, :] > at[None, :, None]) & (at[None, None, :] < at[:, None, None])
    weights = jnp.prod(jnp.where(between, decay[None, None, :], 1.0), axis=2)
    return jnp.where(at[None, :] < at[:, None], weights, 0.0)


def solution(mesh):
    from jax.sharding import Mesh

    head_size, group_size = mesh.devices.shape
    sub = 8 if group_size % 8 == 0 else 1
    fine = Mesh(
        mesh.devices.reshape(head_size, group_size // sub, sub), ("head", "ga", "gb")
    )
    group = ("ga", "gb")
    placed = (
        P(group, "head"),
        P(group, "head"),
        P(group, "head"),
        P(group, "head"),
        P(group, "head"),
        P("head", None),
        P(group, "head", None),
        P(),
        P(("head", "ga", "gb"), None),
        P(group, "head"),
        P(group, "head"),
        P(group, "head"),
        P(),
    )
    return jax.shard_map(
        per_device,
        mesh=fine,
        in_specs=placed,
        out_specs=(P(), P(group, "head"), P(group, "head")),
        check_vma=False,
    )
```

```python
import jax
import jax.numpy as jnp
from jax import lax
from jax.sharding import PartitionSpec as P


def layer_norm(stream, width_eps):
    mean_val = jnp.mean(stream, axis=-1, keepdims=True)
    centered = stream - mean_val
    var_val = jnp.mean(centered * centered, axis=-1, keepdims=True)
    return centered / jnp.sqrt(var_val + width_eps)


def per_device(
    query_proj,
    key_proj,
    value_proj,
    gate_proj,
    log_decay,
    out_weight,
    residual,
    norm_gain,
    vocab_weight,
    targets,
    ref_logp,
    response_mask,
    seq_lengths,
):
    highest_precision = lax.Precision.HIGHEST
    head_count = lax.axis_size("head")
    group_count = lax.axis_size(("ga", "gb"))
    head_index = lax.axis_index("head")
    group_index = lax.axis_index(("ga", "gb"))
    tok_count = query_proj.shape[0]
    heads_here = log_decay.shape[1]
    key_width = query_proj.shape[1] // heads_here
    value_width = value_proj.shape[1] // heads_here
    slice_rows = residual.shape[1]
    seq_count = seq_lengths.shape[0]
    vocab_here = vocab_weight.shape[0]
    key_scaling = key_width ** (-0.5)
    starts = jnp.cumsum(seq_lengths) - seq_lengths
    local_pos = jnp.arange(tok_count, dtype=jnp.int32)
    positions = group_index * tok_count + local_pos
    seq_ids = jnp.sum((positions[:, None] >= starts[None, 1:]).astype(jnp.int32), axis=1)
    is_start = jnp.any(positions[:, None] == starts[None, :], axis=1)
    cumulative_decay = jnp.cumsum(log_decay, axis=0)
    same_seq = (seq_ids[:, None] == seq_ids[None, :]) & (local_pos[None, :] <= local_pos[:, None])
    gap_log = cumulative_decay[:, None, :] - cumulative_decay[None, :, :]
    decay_mat = jnp.where(same_seq[:, :, None], jnp.exp(jnp.minimum(gap_log, 0.0)), 0.0)
    query_heads = query_proj.reshape(tok_count, heads_here, key_width)
    key_heads = key_proj.reshape(tok_count, heads_here, key_width)
    value_heads = value_proj.reshape(tok_count, heads_here, value_width)
    raw_scores = jnp.einsum(
        "thd,shd->tsh", query_heads, key_heads, preferred_element_type=jnp.float32
    )
    weights_in = (raw_scores * key_scaling * decay_mat).astype(jnp.bfloat16)
    in_block = jnp.einsum(
        "tsh,shv->thv", weights_in, value_heads, preferred_element_type=jnp.float32
    )
    continuation_flags = (seq_ids == seq_ids[0]) & jnp.logical_not(is_start[0])
    final_decay_weight = jnp.where(
        (seq_ids == seq_ids[-1])[:, None],
        jnp.exp(cumulative_decay[-1][None, :] - cumulative_decay),
        0.0,
    )
    key_as_float = key_heads.astype(jnp.float32)
    value_as_float = value_heads.astype(jnp.float32)
    block_total_sum = jnp.einsum(
        "ane,anl->nel",
        key_as_float * final_decay_weight[:, :, None],
        value_as_float,
        precision=highest_precision,
    )
    block_decay = jnp.where(jnp.all(continuation_flags), jnp.exp(cumulative_decay[-1]), 0.0)

    assert heads_here == 1
    sub = lax.axis_size("gb")
    part_count = lax.axis_size("ga")
    state_size = key_width * value_width
    pad = jnp.zeros((127,), jnp.float32)
    chunk = state_size // sub
    extras = jnp.concatenate([block_decay, pad])
    payload = jnp.concatenate(
        [
            block_total_sum.reshape(sub, chunk),
            jnp.broadcast_to(extras[None, :], (sub, 128)),
        ],
        axis=1,
    )
    received = lax.all_to_all(payload, "gb", 0, 0, tiled=True)
    slices_in = received[:, :chunk]
    decay_in = received[:, chunk]
    local_in = jnp.dot(decay_weights(decay_in), slices_in, precision=highest_precision)
    tail_weights = decay_weights(jnp.concatenate([decay_in, jnp.ones((1,), jnp.float32)]))[
        sub, :sub
    ]
    octet_total = jnp.dot(tail_weights, slices_in, precision=highest_precision)
    octet_decay = jnp.prod(decay_in)
    lead_decay = jnp.cumprod(jnp.concatenate([jnp.ones((1,), jnp.float32), decay_in[:-1]]))
    piece = chunk // part_count
    extras = jnp.concatenate([octet_decay[None], pad])
    payload = jnp.concatenate(
        [
            octet_total.reshape(part_count, piece),
            jnp.broadcast_to(extras[None, :], (part_count, 128)),
        ],
        axis=1,
    )
    received = lax.all_to_all(payload, "ga", 0, 0, tiled=True)
    octet_in = jnp.dot(
        decay_weights(received[:, piece]), received[:, :piece], precision=highest_precision
    )
    octet_in = lax.all_to_all(octet_in, "ga", 0, 0, tiled=True).reshape(chunk)
    slices_out = local_in + lead_decay[:, None] * octet_in[None, :]
    carried_state = lax.all_to_all(slices_out, "gb", 0, 0, tiled=True).reshape(
        heads_here, key_width, value_width
    )

    vocab_rows = lax.all_gather(vocab_weight, "ga", axis=0, tiled=True)
    vocab_rows, carried_state = lax.optimization_barrier((vocab_rows, carried_state))
    query_as_float = query_heads.astype(jnp.float32)
    state_contribution = (
        jnp.einsum("ugo,gow->ugw", query_as_float, carried_state, precision=highest_precision)
        * key_scaling
        * (jnp.exp(cumulative_decay) * continuation_flags[:, None].astype(jnp.float32))[:, :, None]
    )
    retained = in_block + state_contribution
    state_norms = jnp.log(
        1.0 + jnp.sqrt(jnp.mean(carried_state * carried_state, axis=(1, 2)) + 1e-06)
    )[None, :]
    normed = layer_norm(retained, 1e-06)
    gate_float = gate_proj.reshape(tok_count, heads_here, value_width).astype(jnp.float32)
    gated_out = (
        (normed * jax.nn.silu(gate_float))
        .astype(jnp.bfloat16)
        .reshape(tok_count, heads_here * value_width)
    )
    branch_parts = jnp.dot(gated_out, out_weight, preferred_element_type=jnp.float32)
    own_branch = jnp.sum(
        lax.all_to_all(
            branch_parts.reshape(head_count, slice_rows, -1), "head", 0, 0, tiled=True
        ),
        axis=0,
    )
    stream = residual[0].astype(jnp.float32) + own_branch
    hidden = (layer_norm(stream, 1e-05) * norm_gain).astype(jnp.bfloat16)

    ga_index = lax.axis_index("ga")
    gb_index = lax.axis_index("gb")
    code = jnp.concatenate([targets[0] // 256, targets[0] % 256]).astype(jnp.bfloat16)
    code_row = jnp.pad(code, (0, hidden.shape[1] - code.shape[0]))[None, :]
    hidden_ext = jnp.concatenate([hidden, code_row], axis=0)
    gathered = lax.all_gather(lax.all_gather(hidden_ext, "gb"), "head")
    code_all = gathered[:, :, slice_rows, : 2 * slice_rows].astype(jnp.int32)
    all_targets = (code_all[..., :slice_rows] * 256 + code_all[..., slice_rows:]).reshape(-1)
    entry_ids = (
        (
            head_index * group_count
            + jnp.arange(part_count, dtype=jnp.int32)[:, None] * sub
            + gb_index
        )
        * vocab_here
        + jnp.arange(vocab_here, dtype=jnp.int32)[None, :]
    ).reshape(-1)
    logits = lax.dot_general(
        gathered.reshape(-1, hidden.shape[1]),
        vocab_rows,
        (((1,), (1,)), ((), ())),
        preferred_element_type=jnp.float32,
    ).reshape(head_count * sub, slice_rows + 1, -1)[:, :slice_rows, :].reshape(
        head_count * sub * slice_rows, -1
    )
    top = jnp.max(logits, axis=1)
    exp_total = jnp.sum(jnp.exp(logits - top[:, None]), axis=1)
    picked = jnp.sum(jnp.where(entry_ids[None, :] == all_targets[:, None], logits, 0.0), axis=1)
    outgoing = jnp.stack([top, exp_total, picked]).reshape(3, head_count, sub, slice_rows)
    outgoing = jnp.transpose(outgoing, (1, 2, 0, 3)).reshape(head_count * sub, 3 * slice_rows)
    incoming = lax.all_to_all(outgoing, ("head", "gb"), 0, 0, tiled=True).reshape(
        head_count * sub, 3, slice_rows
    )
    own_max = jnp.max(incoming[:, 0], axis=0)
    own_total = jnp.sum(incoming[:, 1] * jnp.exp(incoming[:, 0] - own_max[None, :]), axis=0)
    own_target = jnp.sum(incoming[:, 2], axis=0)
    token_logp = own_target - own_max - jnp.log(own_total)
    token_ratio = response_mask[0].astype(jnp.float32) * (token_logp - ref_logp[0])
    own_positions = positions[0] + head_index * slice_rows + jnp.arange(slice_rows, dtype=jnp.int32)
    own_seq = jnp.sum((own_positions[:, None] >= starts[None, 1:]).astype(jnp.int32), axis=1)
    member = (own_seq[:, None] == jnp.arange(seq_count, dtype=jnp.int32)[None, :]).astype(
        jnp.float32
    )
    partial_sums = jnp.sum(member * token_ratio[:, None], axis=0)
    seq_total = partial_sums
    for axes in (("head", "gb"), "ga"):
        width = lax.axis_size(axes)
        spread = jnp.broadcast_to(seq_total[None, :], (width, seq_count))
        seq_total = jnp.sum(lax.all_to_all(spread, axes, 0, 0, tiled=True), axis=0)
    seq_ratio = seq_total / seq_lengths.astype(jnp.float32)
    return (seq_ratio, state_norms, own_max[None, :])


def decay_weights(decay):
    count = decay.shape[0]
    at = jnp.arange(count, dtype=jnp.int32)
    between = (at[None, None, :] > at[None, :, None]) & (at[None, None, :] < at[:, None, None])
    weights = jnp.prod(jnp.where(between, decay[None, None, :], 1.0), axis=2)
    return jnp.where(at[None, :] < at[:, None], weights, 0.0)


def solution(mesh):
    from jax.sharding import Mesh

    head_size, group_size = mesh.devices.shape
    sub = 8 if group_size % 8 == 0 else 1
    fine = Mesh(
        mesh.devices.reshape(head_size, group_size // sub, sub), ("head", "ga", "gb")
    )
    group = ("ga", "gb")
    placed = (
        P(group, "head"),
        P(group, "head"),
        P(group, "head"),
        P(group, "head"),
        P(group, "head"),
        P("head", None),
        P(group, "head", None),
        P(),
        P(("head", "ga", "gb"), None),
        P(group, "head"),
        P(group, "head"),
        P(group, "head"),
        P(),
    )
    return jax.shard_map(
        per_device,
        mesh=fine,
        in_specs=placed,
        out_specs=(P(), P(group, "head"), P(group, "head")),
        check_vma=False,
    )
```

```python
import jax
import jax.numpy as jnp
from jax import lax
from jax.sharding import PartitionSpec as P


def layer_norm(stream, width_eps):
    mean_val = jnp.mean(stream, axis=-1, keepdims=True)
    centered = stream - mean_val
    var_val = jnp.mean(centered * centered, axis=-1, keepdims=True)
    return centered / jnp.sqrt(var_val + width_eps)


def per_device(
    query_proj,
    key_proj,
    value_proj,
    gate_proj,
    log_decay,
    out_weight,
    residual,
    norm_gain,
    vocab_weight,
    targets,
    ref_logp,
    response_mask,
    seq_lengths,
):
    highest_precision = lax.Precision.HIGHEST
    head_count = lax.axis_size("head")
    group_count = lax.axis_size(("ga", "gb"))
    head_index = lax.axis_index("head")
    group_index = lax.axis_index(("ga", "gb"))
    tok_count = query_proj.shape[0]
    heads_here = log_decay.shape[1]
    key_width = query_proj.shape[1] // heads_here
    value_width = value_proj.shape[1] // heads_here
    slice_rows = residual.shape[1]
    seq_count = seq_lengths.shape[0]
    vocab_here = vocab_weight.shape[0]
    key_scaling = key_width ** (-0.5)
    starts = jnp.cumsum(seq_lengths) - seq_lengths
    local_pos = jnp.arange(tok_count, dtype=jnp.int32)
    positions = group_index * tok_count + local_pos
    seq_ids = jnp.sum((positions[:, None] >= starts[None, 1:]).astype(jnp.int32), axis=1)
    is_start = jnp.any(positions[:, None] == starts[None, :], axis=1)
    cumulative_decay = jnp.cumsum(log_decay, axis=0)
    same_seq = (seq_ids[:, None] == seq_ids[None, :]) & (local_pos[None, :] <= local_pos[:, None])
    gap_log = cumulative_decay[:, None, :] - cumulative_decay[None, :, :]
    decay_mat = jnp.where(same_seq[:, :, None], jnp.exp(jnp.minimum(gap_log, 0.0)), 0.0)
    query_heads = query_proj.reshape(tok_count, heads_here, key_width)
    key_heads = key_proj.reshape(tok_count, heads_here, key_width)
    value_heads = value_proj.reshape(tok_count, heads_here, value_width)
    raw_scores = jnp.einsum(
        "thd,shd->tsh", query_heads, key_heads, preferred_element_type=jnp.float32
    )
    weights_in = (raw_scores * key_scaling * decay_mat).astype(jnp.bfloat16)
    in_block = jnp.einsum(
        "tsh,shv->thv", weights_in, value_heads, preferred_element_type=jnp.float32
    )
    continuation_flags = (seq_ids == seq_ids[0]) & jnp.logical_not(is_start[0])
    final_decay_weight = jnp.where(
        (seq_ids == seq_ids[-1])[:, None],
        jnp.exp(cumulative_decay[-1][None, :] - cumulative_decay),
        0.0,
    )
    key_as_float = key_heads.astype(jnp.float32)
    value_as_float = value_heads.astype(jnp.float32)
    block_total_sum = jnp.einsum(
        "ane,anl->nel",
        key_as_float * final_decay_weight[:, :, None],
        value_as_float,
        precision=highest_precision,
    )
    block_decay = jnp.where(jnp.all(continuation_flags), jnp.exp(cumulative_decay[-1]), 0.0)

    assert heads_here == 1
    sub = lax.axis_size("gb")
    part_count = lax.axis_size("ga")
    state_size = key_width * value_width
    pad = jnp.zeros((127,), jnp.float32)
    chunk = state_size // sub
    extras = jnp.concatenate([block_decay, pad])
    payload = jnp.concatenate(
        [
            block_total_sum.reshape(sub, chunk),
            jnp.broadcast_to(extras[None, :], (sub, 128)),
        ],
        axis=1,
    )
    received = lax.all_to_all(payload, "gb", 0, 0, tiled=True)
    slices_in = received[:, :chunk]
    decay_in = received[:, chunk]
    local_in = jnp.dot(decay_weights(decay_in), slices_in, precision=highest_precision)
    tail_weights = decay_weights(jnp.concatenate([decay_in, jnp.ones((1,), jnp.float32)]))[
        sub, :sub
    ]
    octet_total = jnp.dot(tail_weights, slices_in, precision=highest_precision)
    octet_decay = jnp.prod(decay_in)
    lead_decay = jnp.cumprod(jnp.concatenate([jnp.ones((1,), jnp.float32), decay_in[:-1]]))
    piece = chunk // part_count
    extras = jnp.concatenate([octet_decay[None], pad])
    payload = jnp.concatenate(
        [
            octet_total.reshape(part_count, piece),
            jnp.broadcast_to(extras[None, :], (part_count, 128)),
        ],
        axis=1,
    )
    received = lax.all_to_all(payload, "ga", 0, 0, tiled=True)
    octet_in = jnp.dot(
        decay_weights(received[:, piece]), received[:, :piece], precision=highest_precision
    )
    octet_in = lax.all_to_all(octet_in, "ga", 0, 0, tiled=True).reshape(chunk)
    slices_out = local_in + lead_decay[:, None] * octet_in[None, :]
    carried_state = lax.all_to_all(slices_out, "gb", 0, 0, tiled=True).reshape(
        heads_here, key_width, value_width
    )

    vocab_rows = lax.all_gather(vocab_weight, "ga", axis=0, tiled=True)
    vocab_rows, carried_state = lax.optimization_barrier((vocab_rows, carried_state))
    query_as_float = query_heads.astype(jnp.float32)
    state_contribution = (
        jnp.einsum("ugo,gow->ugw", query_as_float, carried_state, precision=highest_precision)
        * key_scaling
        * (jnp.exp(cumulative_decay) * continuation_flags[:, None].astype(jnp.float32))[:, :, None]
    )
    retained = in_block + state_contribution
    state_norms = jnp.log(
        1.0 + jnp.sqrt(jnp.mean(carried_state * carried_state, axis=(1, 2)) + 1e-06)
    )[None, :]
    normed = layer_norm(retained, 1e-06)
    gate_float = gate_proj.reshape(tok_count, heads_here, value_width).astype(jnp.float32)
    gated_out = (
        (normed * jax.nn.silu(gate_float))
        .astype(jnp.bfloat16)
        .reshape(tok_count, heads_here * value_width)
    )
    branch_parts = jnp.dot(gated_out, out_weight, preferred_element_type=jnp.float32)
    own_branch = jnp.sum(
        lax.all_to_all(
            branch_parts.reshape(head_count, slice_rows, -1), "head", 0, 0, tiled=True
        ),
        axis=0,
    )
    stream = residual[0].astype(jnp.float32) + own_branch
    hidden = (layer_norm(stream, 1e-05) * norm_gain).astype(jnp.bfloat16)

    ga_index = lax.axis_index("ga")
    gb_index = lax.axis_index("gb")
    code = jnp.concatenate([targets[0] // 256, targets[0] % 256]).astype(jnp.bfloat16)
    code_row = jnp.pad(code, (0, hidden.shape[1] - code.shape[0]))[None, :]
    hidden_ext = jnp.concatenate([hidden, code_row], axis=0)
    spread = jnp.broadcast_to(hidden_ext[None], (sub,) + hidden_ext.shape)
    gathered = lax.all_gather(lax.all_to_all(spread, "gb", 0, 0, tiled=True), "head")
    code_all = gathered[:, :, slice_rows, : 2 * slice_rows].astype(jnp.int32)
    all_targets = (code_all[..., :slice_rows] * 256 + code_all[..., slice_rows:]).reshape(-1)
    entry_ids = (
        (
            head_index * group_count
            + jnp.arange(part_count, dtype=jnp.int32)[:, None] * sub
            + gb_index
        )
        * vocab_here
        + jnp.arange(vocab_here, dtype=jnp.int32)[None, :]
    ).reshape(-1)
    logits = lax.dot_general(
        gathered.reshape(-1, hidden.shape[1]),
        vocab_rows,
        (((1,), (1,)), ((), ())),
        preferred_element_type=jnp.float32,
    ).reshape(head_count * sub, slice_rows + 1, -1)[:, :slice_rows, :].reshape(
        head_count * sub * slice_rows, -1
    )
    top = jnp.max(logits, axis=1)
    exp_total = jnp.sum(jnp.exp(logits - top[:, None]), axis=1)
    picked = jnp.sum(jnp.where(entry_ids[None, :] == all_targets[:, None], logits, 0.0), axis=1)
    outgoing = jnp.stack([top, exp_total, picked]).reshape(3, head_count, sub, slice_rows)
    outgoing = jnp.transpose(outgoing, (1, 2, 0, 3)).reshape(head_count * sub, 3 * slice_rows)
    incoming = lax.all_to_all(outgoing, ("head", "gb"), 0, 0, tiled=True).reshape(
        head_count * sub, 3, slice_rows
    )
    own_max = jnp.max(incoming[:, 0], axis=0)
    own_total = jnp.sum(incoming[:, 1] * jnp.exp(incoming[:, 0] - own_max[None, :]), axis=0)
    own_target = jnp.sum(incoming[:, 2], axis=0)
    token_logp = own_target - own_max - jnp.log(own_total)
    token_ratio = response_mask[0].astype(jnp.float32) * (token_logp - ref_logp[0])
    own_positions = positions[0] + head_index * slice_rows + jnp.arange(slice_rows, dtype=jnp.int32)
    own_seq = jnp.sum((own_positions[:, None] >= starts[None, 1:]).astype(jnp.int32), axis=1)
    member = (own_seq[:, None] == jnp.arange(seq_count, dtype=jnp.int32)[None, :]).astype(
        jnp.float32
    )
    partial_sums = jnp.sum(member * token_ratio[:, None], axis=0)
    seq_total = partial_sums
    for axes in (("head", "gb"), "ga"):
        width = lax.axis_size(axes)
        spread = jnp.broadcast_to(seq_total[None, :], (width, seq_count))
        seq_total = jnp.sum(lax.all_to_all(spread, axes, 0, 0, tiled=True), axis=0)
    seq_ratio = seq_total / seq_lengths.astype(jnp.float32)
    return (seq_ratio, state_norms, own_max[None, :])


def decay_weights(decay):
    count = decay.shape[0]
    at = jnp.arange(count, dtype=jnp.int32)
    between = (at[None, None, :] > at[None, :, None]) & (at[None, None, :] < at[:, None, None])
    weights = jnp.prod(jnp.where(between, decay[None, None, :], 1.0), axis=2)
    return jnp.where(at[None, :] < at[:, None], weights, 0.0)


def solution(mesh):
    from jax.sharding import Mesh

    head_size, group_size = mesh.devices.shape
    sub = 8 if group_size % 8 == 0 else 1
    fine = Mesh(
        mesh.devices.reshape(head_size, group_size // sub, sub), ("head", "ga", "gb")
    )
    group = ("ga", "gb")
    placed = (
        P(group, "head"),
        P(group, "head"),
        P(group, "head"),
        P(group, "head"),
        P(group, "head"),
        P("head", None),
        P(group, "head", None),
        P(),
        P(("head", "ga", "gb"), None),
        P(group, "head"),
        P(group, "head"),
        P(group, "head"),
        P(),
    )
    return jax.shard_map(
        per_device,
        mesh=fine,
        in_specs=placed,
        out_specs=(P(), P(group, "head"), P(group, "head")),
        check_vma=False,
    )
```

```python
import jax
import jax.numpy as jnp
from jax import lax
from jax.sharding import PartitionSpec as P


def layer_norm(stream, width_eps):
    mean_val = jnp.mean(stream, axis=-1, keepdims=True)
    centered = stream - mean_val
    var_val = jnp.mean(centered * centered, axis=-1, keepdims=True)
    return centered / jnp.sqrt(var_val + width_eps)


def per_device(
    query_proj,
    key_proj,
    value_proj,
    gate_proj,
    log_decay,
    out_weight,
    residual,
    norm_gain,
    vocab_weight,
    targets,
    ref_logp,
    response_mask,
    seq_lengths,
):
    highest_precision = lax.Precision.HIGHEST
    head_count = lax.axis_size("head")
    group_count = lax.axis_size(("ga", "gb"))
    head_index = lax.axis_index("head")
    group_index = lax.axis_index(("ga", "gb"))
    tok_count = query_proj.shape[0]
    heads_here = log_decay.shape[1]
    key_width = query_proj.shape[1] // heads_here
    value_width = value_proj.shape[1] // heads_here
    slice_rows = residual.shape[1]
    seq_count = seq_lengths.shape[0]
    vocab_here = vocab_weight.shape[0]
    key_scaling = key_width ** (-0.5)
    starts = jnp.cumsum(seq_lengths) - seq_lengths
    local_pos = jnp.arange(tok_count, dtype=jnp.int32)
    positions = group_index * tok_count + local_pos
    seq_ids = jnp.sum((positions[:, None] >= starts[None, 1:]).astype(jnp.int32), axis=1)
    is_start = jnp.any(positions[:, None] == starts[None, :], axis=1)
    cumulative_decay = jnp.cumsum(log_decay, axis=0)
    same_seq = (seq_ids[:, None] == seq_ids[None, :]) & (local_pos[None, :] <= local_pos[:, None])
    gap_log = cumulative_decay[:, None, :] - cumulative_decay[None, :, :]
    decay_mat = jnp.where(same_seq[:, :, None], jnp.exp(jnp.minimum(gap_log, 0.0)), 0.0)
    query_heads = query_proj.reshape(tok_count, heads_here, key_width)
    key_heads = key_proj.reshape(tok_count, heads_here, key_width)
    value_heads = value_proj.reshape(tok_count, heads_here, value_width)
    raw_scores = jnp.einsum(
        "thd,shd->tsh", query_heads, key_heads, preferred_element_type=jnp.float32
    )
    weights_in = (raw_scores * key_scaling * decay_mat).astype(jnp.bfloat16)
    in_block = jnp.einsum(
        "tsh,shv->thv", weights_in, value_heads, preferred_element_type=jnp.float32
    )
    continuation_flags = (seq_ids == seq_ids[0]) & jnp.logical_not(is_start[0])
    final_decay_weight = jnp.where(
        (seq_ids == seq_ids[-1])[:, None],
        jnp.exp(cumulative_decay[-1][None, :] - cumulative_decay),
        0.0,
    )
    key_as_float = key_heads.astype(jnp.float32)
    value_as_float = value_heads.astype(jnp.float32)
    block_total_sum = jnp.einsum(
        "ane,anl->nel",
        key_as_float * final_decay_weight[:, :, None],
        value_as_float,
        precision=highest_precision,
    )
    block_decay = jnp.where(jnp.all(continuation_flags), jnp.exp(cumulative_decay[-1]), 0.0)

    assert heads_here == 1
    sub = lax.axis_size("gb")
    part_count = lax.axis_size("ga")
    state_size = key_width * value_width
    pad = jnp.zeros((127,), jnp.float32)
    chunk = state_size // sub
    extras = jnp.concatenate([block_decay, pad])
    payload = jnp.concatenate(
        [
            block_total_sum.reshape(sub, chunk),
            jnp.broadcast_to(extras[None, :], (sub, 128)),
        ],
        axis=1,
    )
    received = lax.all_to_all(payload, "gb", 0, 0, tiled=True)
    slices_in = received[:, :chunk]
    decay_in = received[:, chunk]
    local_in = jnp.dot(decay_weights(decay_in), slices_in, precision=highest_precision)
    tail_weights = decay_weights(jnp.concatenate([decay_in, jnp.ones((1,), jnp.float32)]))[
        sub, :sub
    ]
    octet_total = jnp.dot(tail_weights, slices_in, precision=highest_precision)
    octet_decay = jnp.prod(decay_in)
    lead_decay = jnp.cumprod(jnp.concatenate([jnp.ones((1,), jnp.float32), decay_in[:-1]]))
    piece = chunk // part_count
    extras = jnp.concatenate([octet_decay[None], pad])
    payload = jnp.concatenate(
        [
            octet_total.reshape(part_count, piece),
            jnp.broadcast_to(extras[None, :], (part_count, 128)),
        ],
        axis=1,
    )
    received = lax.all_to_all(payload, "ga", 0, 0, tiled=True)
    octet_in = jnp.dot(
        decay_weights(received[:, piece]), received[:, :piece], precision=highest_precision
    )
    octet_in = lax.all_to_all(octet_in, "ga", 0, 0, tiled=True).reshape(chunk)
    slices_out = local_in + lead_decay[:, None] * octet_in[None, :]
    carried_state = lax.all_to_all(slices_out, "gb", 0, 0, tiled=True).reshape(
        heads_here, key_width, value_width
    )

    vocab_rows = lax.all_gather(vocab_weight, "ga", axis=0, tiled=True)
    query_as_float = query_heads.astype(jnp.float32)
    state_contribution = (
        jnp.einsum("ugo,gow->ugw", query_as_float, carried_state, precision=highest_precision)
        * key_scaling
        * (jnp.exp(cumulative_decay) * continuation_flags[:, None].astype(jnp.float32))[:, :, None]
    )
    retained = in_block + state_contribution
    state_norms = jnp.log(
        1.0 + jnp.sqrt(jnp.mean(carried_state * carried_state, axis=(1, 2)) + 1e-06)
    )[None, :]
    normed = layer_norm(retained, 1e-06)
    gate_float = gate_proj.reshape(tok_count, heads_here, value_width).astype(jnp.float32)
    gated_out = (
        (normed * jax.nn.silu(gate_float))
        .astype(jnp.bfloat16)
        .reshape(tok_count, heads_here * value_width)
    )
    branch_parts = jnp.dot(gated_out, out_weight, preferred_element_type=jnp.float32)
    own_branch = jnp.sum(
        lax.all_to_all(
            branch_parts.reshape(head_count, slice_rows, -1), "head", 0, 0, tiled=True
        ),
        axis=0,
    )
    vocab_rows, own_branch = lax.optimization_barrier((vocab_rows, own_branch))
    stream = residual[0].astype(jnp.float32) + own_branch
    hidden = (layer_norm(stream, 1e-05) * norm_gain).astype(jnp.bfloat16)

    ga_index = lax.axis_index("ga")
    gb_index = lax.axis_index("gb")
    code = jnp.concatenate([targets[0] // 256, targets[0] % 256]).astype(jnp.bfloat16)
    code_row = jnp.pad(code, (0, hidden.shape[1] - code.shape[0]))[None, :]
    hidden_ext = jnp.concatenate([hidden, code_row], axis=0)
    spread = jnp.broadcast_to(hidden_ext[None], (sub,) + hidden_ext.shape)
    gathered = lax.all_gather(lax.all_to_all(spread, "gb", 0, 0, tiled=True), "head")
    code_all = gathered[:, :, slice_rows, : 2 * slice_rows].astype(jnp.int32)
    all_targets = (code_all[..., :slice_rows] * 256 + code_all[..., slice_rows:]).reshape(-1)
    entry_ids = (
        (
            head_index * group_count
            + jnp.arange(part_count, dtype=jnp.int32)[:, None] * sub
            + gb_index
        )
        * vocab_here
        + jnp.arange(vocab_here, dtype=jnp.int32)[None, :]
    ).reshape(-1)
    logits = lax.dot_general(
        gathered.reshape(-1, hidden.shape[1]),
        vocab_rows,
        (((1,), (1,)), ((), ())),
        preferred_element_type=jnp.float32,
    ).reshape(head_count * sub, slice_rows + 1, -1)[:, :slice_rows, :].reshape(
        head_count * sub * slice_rows, -1
    )
    top = jnp.max(logits, axis=1)
    exp_total = jnp.sum(jnp.exp(logits - top[:, None]), axis=1)
    picked = jnp.sum(jnp.where(entry_ids[None, :] == all_targets[:, None], logits, 0.0), axis=1)
    outgoing = jnp.stack([top, exp_total, picked]).reshape(3, head_count, sub, slice_rows)
    outgoing = jnp.transpose(outgoing, (1, 2, 0, 3)).reshape(head_count * sub, 3 * slice_rows)
    incoming = lax.all_to_all(outgoing, ("head", "gb"), 0, 0, tiled=True).reshape(
        head_count * sub, 3, slice_rows
    )
    own_max = jnp.max(incoming[:, 0], axis=0)
    own_total = jnp.sum(incoming[:, 1] * jnp.exp(incoming[:, 0] - own_max[None, :]), axis=0)
    own_target = jnp.sum(incoming[:, 2], axis=0)
    token_logp = own_target - own_max - jnp.log(own_total)
    token_ratio = response_mask[0].astype(jnp.float32) * (token_logp - ref_logp[0])
    own_positions = positions[0] + head_index * slice_rows + jnp.arange(slice_rows, dtype=jnp.int32)
    own_seq = jnp.sum((own_positions[:, None] >= starts[None, 1:]).astype(jnp.int32), axis=1)
    member = (own_seq[:, None] == jnp.arange(seq_count, dtype=jnp.int32)[None, :]).astype(
        jnp.float32
    )
    partial_sums = jnp.sum(member * token_ratio[:, None], axis=0)
    seq_total = partial_sums
    for axes in (("head", "gb"), "ga"):
        width = lax.axis_size(axes)
        spread = jnp.broadcast_to(seq_total[None, :], (width, seq_count))
        seq_total = jnp.sum(lax.all_to_all(spread, axes, 0, 0, tiled=True), axis=0)
    seq_ratio = seq_total / seq_lengths.astype(jnp.float32)
    return (seq_ratio, state_norms, own_max[None, :])


def decay_weights(decay):
    count = decay.shape[0]
    at = jnp.arange(count, dtype=jnp.int32)
    between = (at[None, None, :] > at[None, :, None]) & (at[None, None, :] < at[:, None, None])
    weights = jnp.prod(jnp.where(between, decay[None, None, :], 1.0), axis=2)
    return jnp.where(at[None, :] < at[:, None], weights, 0.0)


def solution(mesh):
    from jax.sharding import Mesh

    head_size, group_size = mesh.devices.shape
    sub = 8 if group_size % 8 == 0 else 1
    fine = Mesh(
        mesh.devices.reshape(head_size, group_size // sub, sub), ("head", "ga", "gb")
    )
    group = ("ga", "gb")
    placed = (
        P(group, "head"),
        P(group, "head"),
        P(group, "head"),
        P(group, "head"),
        P(group, "head"),
        P("head", None),
        P(group, "head", None),
        P(),
        P(("head", "ga", "gb"), None),
        P(group, "head"),
        P(group, "head"),
        P(group, "head"),
        P(),
    )
    return jax.shard_map(
        per_device,
        mesh=fine,
        in_specs=placed,
        out_specs=(P(), P(group, "head"), P(group, "head")),
        check_vma=False,
    )
```

```python
import jax
import jax.numpy as jnp
from jax import lax
from jax.sharding import PartitionSpec as P


def layer_norm(stream, width_eps):
    mean_val = jnp.mean(stream, axis=-1, keepdims=True)
    centered = stream - mean_val
    var_val = jnp.mean(centered * centered, axis=-1, keepdims=True)
    return centered / jnp.sqrt(var_val + width_eps)


def per_device(
    query_proj,
    key_proj,
    value_proj,
    gate_proj,
    log_decay,
    out_weight,
    residual,
    norm_gain,
    vocab_weight,
    targets,
    ref_logp,
    response_mask,
    seq_lengths,
):
    highest_precision = lax.Precision.HIGHEST
    head_count = lax.axis_size("head")
    group_count = lax.axis_size(("ga", "gb"))
    head_index = lax.axis_index("head")
    group_index = lax.axis_index(("ga", "gb"))
    tok_count = query_proj.shape[0]
    heads_here = log_decay.shape[1]
    key_width = query_proj.shape[1] // heads_here
    value_width = value_proj.shape[1] // heads_here
    slice_rows = residual.shape[1]
    seq_count = seq_lengths.shape[0]
    vocab_here = vocab_weight.shape[0]
    key_scaling = key_width ** (-0.5)
    starts = jnp.cumsum(seq_lengths) - seq_lengths
    local_pos = jnp.arange(tok_count, dtype=jnp.int32)
    positions = group_index * tok_count + local_pos
    seq_ids = jnp.sum((positions[:, None] >= starts[None, 1:]).astype(jnp.int32), axis=1)
    is_start = jnp.any(positions[:, None] == starts[None, :], axis=1)
    cumulative_decay = jnp.cumsum(log_decay, axis=0)
    same_seq = (seq_ids[:, None] == seq_ids[None, :]) & (local_pos[None, :] <= local_pos[:, None])
    gap_log = cumulative_decay[:, None, :] - cumulative_decay[None, :, :]
    decay_mat = jnp.where(same_seq[:, :, None], jnp.exp(jnp.minimum(gap_log, 0.0)), 0.0)
    query_heads = query_proj.reshape(tok_count, heads_here, key_width)
    key_heads = key_proj.reshape(tok_count, heads_here, key_width)
    value_heads = value_proj.reshape(tok_count, heads_here, value_width)
    raw_scores = jnp.einsum(
        "thd,shd->tsh", query_heads, key_heads, preferred_element_type=jnp.float32
    )
    weights_in = (raw_scores * key_scaling * decay_mat).astype(jnp.bfloat16)
    in_block = jnp.einsum(
        "tsh,shv->thv", weights_in, value_heads, preferred_element_type=jnp.float32
    )
    continuation_flags = (seq_ids == seq_ids[0]) & jnp.logical_not(is_start[0])
    final_decay_weight = jnp.where(
        (seq_ids == seq_ids[-1])[:, None],
        jnp.exp(cumulative_decay[-1][None, :] - cumulative_decay),
        0.0,
    )
    key_as_float = key_heads.astype(jnp.float32)
    value_as_float = value_heads.astype(jnp.float32)
    block_total_sum = jnp.einsum(
        "ane,anl->nel",
        key_as_float * final_decay_weight[:, :, None],
        value_as_float,
        precision=highest_precision,
    )
    block_decay = jnp.where(jnp.all(continuation_flags), jnp.exp(cumulative_decay[-1]), 0.0)

    assert heads_here == 1
    sub = lax.axis_size("gb")
    part_count = lax.axis_size("ga")
    state_size = key_width * value_width
    pad = jnp.zeros((127,), jnp.float32)
    chunk = state_size // sub
    extras = jnp.concatenate([block_decay, pad])
    payload = jnp.concatenate(
        [
            block_total_sum.reshape(sub, chunk),
            jnp.broadcast_to(extras[None, :], (sub, 128)),
        ],
        axis=1,
    )
    received = lax.all_to_all(payload, "gb", 0, 0, tiled=True)
    slices_in = received[:, :chunk]
    decay_in = received[:, chunk]
    local_in = jnp.dot(decay_weights(decay_in), slices_in, precision=highest_precision)
    tail_weights = decay_weights(jnp.concatenate([decay_in, jnp.ones((1,), jnp.float32)]))[
        sub, :sub
    ]
    octet_total = jnp.dot(tail_weights, slices_in, precision=highest_precision)
    octet_decay = jnp.prod(decay_in)
    lead_decay = jnp.cumprod(jnp.concatenate([jnp.ones((1,), jnp.float32), decay_in[:-1]]))
    extras = jnp.concatenate([octet_decay[None], pad])
    payload = jnp.concatenate([octet_total, extras])
    received = lax.all_to_all(
        jnp.broadcast_to(payload[None, :], (part_count,) + payload.shape), "ga", 0, 0, tiled=True
    )
    octet_in = jnp.dot(
        decay_weights(received[:, chunk])[lax.axis_index("ga")],
        received[:, :chunk],
        precision=highest_precision,
    )
    slices_out = local_in + lead_decay[:, None] * octet_in[None, :]
    carried_state = lax.all_to_all(slices_out, "gb", 0, 0, tiled=True).reshape(
        heads_here, key_width, value_width
    )

    vocab_rows = lax.all_gather(vocab_weight, "ga", axis=0, tiled=True)
    query_as_float = query_heads.astype(jnp.float32)
    state_contribution = (
        jnp.einsum("ugo,gow->ugw", query_as_float, carried_state, precision=highest_precision)
        * key_scaling
        * (jnp.exp(cumulative_decay) * continuation_flags[:, None].astype(jnp.float32))[:, :, None]
    )
    retained = in_block + state_contribution
    state_norms = jnp.log(
        1.0 + jnp.sqrt(jnp.mean(carried_state * carried_state, axis=(1, 2)) + 1e-06)
    )[None, :]
    normed = layer_norm(retained, 1e-06)
    gate_float = gate_proj.reshape(tok_count, heads_here, value_width).astype(jnp.float32)
    gated_out = (
        (normed * jax.nn.silu(gate_float))
        .astype(jnp.bfloat16)
        .reshape(tok_count, heads_here * value_width)
    )
    branch_parts = jnp.dot(gated_out, out_weight, preferred_element_type=jnp.float32)
    own_branch = jnp.sum(
        lax.all_to_all(
            branch_parts.reshape(head_count, slice_rows, -1), "head", 0, 0, tiled=True
        ),
        axis=0,
    )
    vocab_rows, own_branch = lax.optimization_barrier((vocab_rows, own_branch))
    stream = residual[0].astype(jnp.float32) + own_branch
    hidden = (layer_norm(stream, 1e-05) * norm_gain).astype(jnp.bfloat16)

    ga_index = lax.axis_index("ga")
    gb_index = lax.axis_index("gb")
    code = jnp.concatenate([targets[0] // 256, targets[0] % 256]).astype(jnp.bfloat16)
    code_row = jnp.pad(code, (0, hidden.shape[1] - code.shape[0]))[None, :]
    hidden_ext = jnp.concatenate([hidden, code_row], axis=0)
    spread = jnp.broadcast_to(hidden_ext[None], (sub,) + hidden_ext.shape)
    gathered = lax.all_gather(lax.all_to_all(spread, "gb", 0, 0, tiled=True), "head")
    code_all = gathered[:, :, slice_rows, : 2 * slice_rows].astype(jnp.int32)
    all_targets = (code_all[..., :slice_rows] * 256 + code_all[..., slice_rows:]).reshape(-1)
    entry_ids = (
        (
            head_index * group_count
            + jnp.arange(part_count, dtype=jnp.int32)[:, None] * sub
            + gb_index
        )
        * vocab_here
        + jnp.arange(vocab_here, dtype=jnp.int32)[None, :]
    ).reshape(-1)
    logits = lax.dot_general(
        gathered.reshape(-1, hidden.shape[1]),
        vocab_rows,
        (((1,), (1,)), ((), ())),
        preferred_element_type=jnp.float32,
    ).reshape(head_count * sub, slice_rows + 1, -1)[:, :slice_rows, :].reshape(
        head_count * sub * slice_rows, -1
    )
    top = jnp.max(logits, axis=1)
    exp_total = jnp.sum(jnp.exp(logits - top[:, None]), axis=1)
    picked = jnp.sum(jnp.where(entry_ids[None, :] == all_targets[:, None], logits, 0.0), axis=1)
    outgoing = jnp.stack([top, exp_total, picked]).reshape(3, head_count, sub, slice_rows)
    outgoing = jnp.transpose(outgoing, (1, 2, 0, 3)).reshape(head_count * sub, 3 * slice_rows)
    incoming = lax.all_to_all(outgoing, ("head", "gb"), 0, 0, tiled=True).reshape(
        head_count * sub, 3, slice_rows
    )
    own_max = jnp.max(incoming[:, 0], axis=0)
    own_total = jnp.sum(incoming[:, 1] * jnp.exp(incoming[:, 0] - own_max[None, :]), axis=0)
    own_target = jnp.sum(incoming[:, 2], axis=0)
    token_logp = own_target - own_max - jnp.log(own_total)
    token_ratio = response_mask[0].astype(jnp.float32) * (token_logp - ref_logp[0])
    own_positions = positions[0] + head_index * slice_rows + jnp.arange(slice_rows, dtype=jnp.int32)
    own_seq = jnp.sum((own_positions[:, None] >= starts[None, 1:]).astype(jnp.int32), axis=1)
    member = (own_seq[:, None] == jnp.arange(seq_count, dtype=jnp.int32)[None, :]).astype(
        jnp.float32
    )
    partial_sums = jnp.sum(member * token_ratio[:, None], axis=0)
    seq_total = partial_sums
    for axes in (("head", "gb"), "ga"):
        width = lax.axis_size(axes)
        spread = jnp.broadcast_to(seq_total[None, :], (width, seq_count))
        seq_total = jnp.sum(lax.all_to_all(spread, axes, 0, 0, tiled=True), axis=0)
    seq_ratio = seq_total / seq_lengths.astype(jnp.float32)
    return (seq_ratio, state_norms, own_max[None, :])


def decay_weights(decay):
    count = decay.shape[0]
    at = jnp.arange(count, dtype=jnp.int32)
    between = (at[None, None, :] > at[None, :, None]) & (at[None, None, :] < at[:, None, None])
    weights = jnp.prod(jnp.where(between, decay[None, None, :], 1.0), axis=2)
    return jnp.where(at[None, :] < at[:, None], weights, 0.0)


def solution(mesh):
    from jax.sharding import Mesh

    head_size, group_size = mesh.devices.shape
    sub = 8 if group_size % 8 == 0 else 1
    fine = Mesh(
        mesh.devices.reshape(head_size, group_size // sub, sub), ("head", "ga", "gb")
    )
    group = ("ga", "gb")
    placed = (
        P(group, "head"),
        P(group, "head"),
        P(group, "head"),
        P(group, "head"),
        P(group, "head"),
        P("head", None),
        P(group, "head", None),
        P(),
        P(("head", "ga", "gb"), None),
        P(group, "head"),
        P(group, "head"),
        P(group, "head"),
        P(),
    )
    return jax.shard_map(
        per_device,
        mesh=fine,
        in_specs=placed,
        out_specs=(P(), P(group, "head"), P(group, "head")),
        check_vma=False,
    )
```

```python
import jax
import jax.numpy as jnp
from jax import lax
from jax.sharding import PartitionSpec as P


def layer_norm(stream, width_eps):
    mean_val = jnp.mean(stream, axis=-1, keepdims=True)
    centered = stream - mean_val
    var_val = jnp.mean(centered * centered, axis=-1, keepdims=True)
    return centered / jnp.sqrt(var_val + width_eps)


def per_device(
    query_proj,
    key_proj,
    value_proj,
    gate_proj,
    log_decay,
    out_weight,
    residual,
    norm_gain,
    vocab_weight,
    targets,
    ref_logp,
    response_mask,
    seq_lengths,
):
    highest_precision = lax.Precision.HIGHEST
    head_count = lax.axis_size("head")
    group_count = lax.axis_size(("ga", "gb"))
    head_index = lax.axis_index("head")
    group_index = lax.axis_index(("ga", "gb"))
    tok_count = query_proj.shape[0]
    heads_here = log_decay.shape[1]
    key_width = query_proj.shape[1] // heads_here
    value_width = value_proj.shape[1] // heads_here
    slice_rows = residual.shape[1]
    seq_count = seq_lengths.shape[0]
    vocab_here = vocab_weight.shape[0]
    key_scaling = key_width ** (-0.5)
    starts = jnp.cumsum(seq_lengths) - seq_lengths
    local_pos = jnp.arange(tok_count, dtype=jnp.int32)
    positions = group_index * tok_count + local_pos
    seq_ids = jnp.sum((positions[:, None] >= starts[None, 1:]).astype(jnp.int32), axis=1)
    is_start = jnp.any(positions[:, None] == starts[None, :], axis=1)
    cumulative_decay = jnp.cumsum(log_decay, axis=0)
    same_seq = (seq_ids[:, None] == seq_ids[None, :]) & (local_pos[None, :] <= local_pos[:, None])
    gap_log = cumulative_decay[:, None, :] - cumulative_decay[None, :, :]
    decay_mat = jnp.where(same_seq[:, :, None], jnp.exp(jnp.minimum(gap_log, 0.0)), 0.0)
    query_heads = query_proj.reshape(tok_count, heads_here, key_width)
    key_heads = key_proj.reshape(tok_count, heads_here, key_width)
    value_heads = value_proj.reshape(tok_count, heads_here, value_width)
    raw_scores = jnp.einsum(
        "thd,shd->tsh", query_heads, key_heads, preferred_element_type=jnp.float32
    )
    weights_in = (raw_scores * key_scaling * decay_mat).astype(jnp.bfloat16)
    in_block = jnp.einsum(
        "tsh,shv->thv", weights_in, value_heads, preferred_element_type=jnp.float32
    )
    continuation_flags = (seq_ids == seq_ids[0]) & jnp.logical_not(is_start[0])
    final_decay_weight = jnp.where(
        (seq_ids == seq_ids[-1])[:, None],
        jnp.exp(cumulative_decay[-1][None, :] - cumulative_decay),
        0.0,
    )
    key_as_float = key_heads.astype(jnp.float32)
    value_as_float = value_heads.astype(jnp.float32)
    block_total_sum = jnp.einsum(
        "ane,anl->nel",
        key_as_float * final_decay_weight[:, :, None],
        value_as_float,
        precision=highest_precision,
    )
    block_decay = jnp.where(jnp.all(continuation_flags), jnp.exp(cumulative_decay[-1]), 0.0)

    assert heads_here == 1
    sub = lax.axis_size("gb")
    part_count = lax.axis_size("ga")
    state_size = key_width * value_width
    pad = jnp.zeros((127,), jnp.float32)
    chunk = state_size // sub
    extras = jnp.concatenate([block_decay, pad])
    payload = jnp.concatenate(
        [
            block_total_sum.reshape(sub, chunk),
            jnp.broadcast_to(extras[None, :], (sub, 128)),
        ],
        axis=1,
    )
    received = lax.all_to_all(payload, "gb", 0, 0, tiled=True)
    slices_in = received[:, :chunk]
    decay_in = received[:, chunk]
    local_in = jnp.dot(decay_weights(decay_in), slices_in, precision=highest_precision)
    tail_weights = decay_weights(jnp.concatenate([decay_in, jnp.ones((1,), jnp.float32)]))[
        sub, :sub
    ]
    octet_total = jnp.dot(tail_weights, slices_in, precision=highest_precision)
    octet_decay = jnp.prod(decay_in)
    lead_decay = jnp.cumprod(jnp.concatenate([jnp.ones((1,), jnp.float32), decay_in[:-1]]))
    piece = chunk // part_count
    extras = jnp.concatenate([octet_decay[None], pad])
    payload = jnp.concatenate(
        [
            octet_total.reshape(part_count, piece),
            jnp.broadcast_to(extras[None, :], (part_count, 128)),
        ],
        axis=1,
    )
    received = lax.all_to_all(payload, "ga", 0, 0, tiled=True)
    octet_in = jnp.dot(
        decay_weights(received[:, piece]), received[:, :piece], precision=highest_precision
    )
    octet_in = lax.all_to_all(octet_in, "ga", 0, 0, tiled=True).reshape(chunk)
    slices_out = local_in + lead_decay[:, None] * octet_in[None, :]
    carried_state = lax.all_to_all(slices_out, "gb", 0, 0, tiled=True).reshape(
        heads_here, key_width, value_width
    )

    vocab_rows = lax.all_gather(vocab_weight, "ga", axis=0, tiled=True)
    query_as_float = query_heads.astype(jnp.float32)
    state_contribution = (
        jnp.einsum("ugo,gow->ugw", query_as_float, carried_state, precision=highest_precision)
        * key_scaling
        * (jnp.exp(cumulative_decay) * continuation_flags[:, None].astype(jnp.float32))[:, :, None]
    )
    retained = in_block + state_contribution
    state_norms = jnp.log(
        1.0 + jnp.sqrt(jnp.mean(carried_state * carried_state, axis=(1, 2)) + 1e-06)
    )[None, :]
    normed = layer_norm(retained, 1e-06)
    gate_float = gate_proj.reshape(tok_count, heads_here, value_width).astype(jnp.float32)
    gated_out = (
        (normed * jax.nn.silu(gate_float))
        .astype(jnp.bfloat16)
        .reshape(tok_count, heads_here * value_width)
    )
    branch_parts = jnp.dot(gated_out, out_weight, preferred_element_type=jnp.float32)
    own_branch = jnp.sum(
        lax.all_to_all(
            branch_parts.reshape(head_count, slice_rows, -1), "head", 0, 0, tiled=True
        ),
        axis=0,
    )
    vocab_rows, own_branch = lax.optimization_barrier((vocab_rows, own_branch))
    stream = residual[0].astype(jnp.float32) + own_branch
    hidden = (layer_norm(stream, 1e-05) * norm_gain).astype(jnp.bfloat16)

    ga_index = lax.axis_index("ga")
    gb_index = lax.axis_index("gb")
    code = jnp.concatenate([targets[0] // 256, targets[0] % 256]).astype(jnp.bfloat16)
    code_row = jnp.pad(code, (0, hidden.shape[1] - code.shape[0]))[None, :]
    hidden_ext = jnp.concatenate([hidden, code_row], axis=0)
    spread = jnp.broadcast_to(hidden_ext[None], (sub,) + hidden_ext.shape)
    gathered = lax.all_gather(lax.all_to_all(spread, "gb", 0, 0, tiled=True), "head")
    code_all = gathered[:, :, slice_rows, : 2 * slice_rows].astype(jnp.int32)
    all_targets = (code_all[..., :slice_rows] * 256 + code_all[..., slice_rows:]).reshape(-1)
    entry_ids = (
        (
            head_index * group_count
            + jnp.arange(part_count, dtype=jnp.int32)[:, None] * sub
            + gb_index
        )
        * vocab_here
        + jnp.arange(vocab_here, dtype=jnp.int32)[None, :]
    ).reshape(-1)
    logits = lax.dot_general(
        gathered.reshape(-1, hidden.shape[1]),
        vocab_rows,
        (((1,), (1,)), ((), ())),
        preferred_element_type=jnp.float32,
    ).reshape(head_count * sub, slice_rows + 1, -1)[:, :slice_rows, :].reshape(
        head_count * sub * slice_rows, -1
    )
    top = jnp.max(logits, axis=1)
    exp_total = jnp.sum(jnp.exp(logits - top[:, None]), axis=1)
    picked = jnp.sum(jnp.where(entry_ids[None, :] == all_targets[:, None], logits, 0.0), axis=1)
    outgoing = jnp.stack([top, exp_total, picked]).reshape(3, head_count, sub, slice_rows)
    outgoing = jnp.transpose(outgoing, (1, 2, 0, 3)).reshape(head_count * sub, 3 * slice_rows)
    incoming = lax.all_to_all(outgoing, ("head", "gb"), 0, 0, tiled=True).reshape(
        head_count * sub, 3, slice_rows
    )
    own_max = jnp.max(incoming[:, 0], axis=0)
    own_total = jnp.sum(incoming[:, 1] * jnp.exp(incoming[:, 0] - own_max[None, :]), axis=0)
    own_target = jnp.sum(incoming[:, 2], axis=0)
    token_logp = own_target - own_max - jnp.log(own_total)
    token_ratio = response_mask[0].astype(jnp.float32) * (token_logp - ref_logp[0])
    own_positions = positions[0] + head_index * slice_rows + jnp.arange(slice_rows, dtype=jnp.int32)
    own_seq = jnp.sum((own_positions[:, None] >= starts[None, 1:]).astype(jnp.int32), axis=1)
    member = (own_seq[:, None] == jnp.arange(seq_count, dtype=jnp.int32)[None, :]).astype(
        jnp.float32
    )
    partial_sums = jnp.sum(member * token_ratio[:, None], axis=0)
    seq_total = partial_sums
    for axes in ("head", ("ga", "gb")):
        width = lax.axis_size(axes)
        spread = jnp.broadcast_to(seq_total[None, :], (width, seq_count))
        seq_total = jnp.sum(lax.all_to_all(spread, axes, 0, 0, tiled=True), axis=0)
    seq_ratio = seq_total / seq_lengths.astype(jnp.float32)
    return (seq_ratio, state_norms, own_max[None, :])


def decay_weights(decay):
    count = decay.shape[0]
    at = jnp.arange(count, dtype=jnp.int32)
    between = (at[None, None, :] > at[None, :, None]) & (at[None, None, :] < at[:, None, None])
    weights = jnp.prod(jnp.where(between, decay[None, None, :], 1.0), axis=2)
    return jnp.where(at[None, :] < at[:, None], weights, 0.0)


def solution(mesh):
    from jax.sharding import Mesh

    head_size, group_size = mesh.devices.shape
    sub = 8 if group_size % 8 == 0 else 1
    fine = Mesh(
        mesh.devices.reshape(head_size, group_size // sub, sub), ("head", "ga", "gb")
    )
    group = ("ga", "gb")
    placed = (
        P(group, "head"),
        P(group, "head"),
        P(group, "head"),
        P(group, "head"),
        P(group, "head"),
        P("head", None),
        P(group, "head", None),
        P(),
        P(("head", "ga", "gb"), None),
        P(group, "head"),
        P(group, "head"),
        P(group, "head"),
        P(),
    )
    return jax.shard_map(
        per_device,
        mesh=fine,
        in_specs=placed,
        out_specs=(P(), P(group, "head"), P(group, "head")),
        check_vma=False,
    )
```

```python
import jax
import jax.numpy as jnp
from jax import lax
from jax.sharding import PartitionSpec as P


def layer_norm(stream, width_eps):
    mean_val = jnp.mean(stream, axis=-1, keepdims=True)
    centered = stream - mean_val
    var_val = jnp.mean(centered * centered, axis=-1, keepdims=True)
    return centered / jnp.sqrt(var_val + width_eps)


def per_device(
    query_proj,
    key_proj,
    value_proj,
    gate_proj,
    log_decay,
    out_weight,
    residual,
    norm_gain,
    vocab_weight,
    targets,
    ref_logp,
    response_mask,
    seq_lengths,
):
    highest_precision = lax.Precision.HIGHEST
    head_count = lax.axis_size("head")
    group_count = lax.axis_size(("ga", "gb"))
    head_index = lax.axis_index("head")
    group_index = lax.axis_index(("ga", "gb"))
    tok_count = query_proj.shape[0]
    heads_here = log_decay.shape[1]
    key_width = query_proj.shape[1] // heads_here
    value_width = value_proj.shape[1] // heads_here
    slice_rows = residual.shape[1]
    seq_count = seq_lengths.shape[0]
    vocab_here = vocab_weight.shape[0]
    key_scaling = key_width ** (-0.5)
    starts = jnp.cumsum(seq_lengths) - seq_lengths
    local_pos = jnp.arange(tok_count, dtype=jnp.int32)
    positions = group_index * tok_count + local_pos
    seq_ids = jnp.sum((positions[:, None] >= starts[None, 1:]).astype(jnp.int32), axis=1)
    is_start = jnp.any(positions[:, None] == starts[None, :], axis=1)
    cumulative_decay = jnp.cumsum(log_decay, axis=0)
    same_seq = (seq_ids[:, None] == seq_ids[None, :]) & (local_pos[None, :] <= local_pos[:, None])
    gap_log = cumulative_decay[:, None, :] - cumulative_decay[None, :, :]
    decay_mat = jnp.where(same_seq[:, :, None], jnp.exp(jnp.minimum(gap_log, 0.0)), 0.0)
    query_heads = query_proj.reshape(tok_count, heads_here, key_width)
    key_heads = key_proj.reshape(tok_count, heads_here, key_width)
    value_heads = value_proj.reshape(tok_count, heads_here, value_width)
    raw_scores = jnp.einsum(
        "thd,shd->tsh", query_heads, key_heads, preferred_element_type=jnp.float32
    )
    weights_in = (raw_scores * key_scaling * decay_mat).astype(jnp.bfloat16)
    in_block = jnp.einsum(
        "tsh,shv->thv", weights_in, value_heads, preferred_element_type=jnp.float32
    )
    continuation_flags = (seq_ids == seq_ids[0]) & jnp.logical_not(is_start[0])
    final_decay_weight = jnp.where(
        (seq_ids == seq_ids[-1])[:, None],
        jnp.exp(cumulative_decay[-1][None, :] - cumulative_decay),
        0.0,
    )
    key_as_float = key_heads.astype(jnp.float32)
    value_as_float = value_heads.astype(jnp.float32)
    block_total_sum = jnp.einsum(
        "ane,anl->nel",
        key_as_float * final_decay_weight[:, :, None],
        value_as_float,
        precision=highest_precision,
    )
    block_decay = jnp.where(jnp.all(continuation_flags), jnp.exp(cumulative_decay[-1]), 0.0)

    assert heads_here == 1
    sub = lax.axis_size("gb")
    part_count = lax.axis_size("ga")
    state_size = key_width * value_width
    pad = jnp.zeros((127,), jnp.float32)
    chunk = state_size // sub
    extras = jnp.concatenate([block_decay, pad])
    payload = jnp.concatenate(
        [
            block_total_sum.reshape(sub, chunk),
            jnp.broadcast_to(extras[None, :], (sub, 128)),
        ],
        axis=1,
    )
    received = lax.all_to_all(payload, "gb", 0, 0, tiled=True)
    slices_in = received[:, :chunk]
    decay_in = received[:, chunk]
    local_in = jnp.dot(decay_weights(decay_in), slices_in, precision=highest_precision)
    tail_weights = decay_weights(jnp.concatenate([decay_in, jnp.ones((1,), jnp.float32)]))[
        sub, :sub
    ]
    octet_total = jnp.dot(tail_weights, slices_in, precision=highest_precision)
    octet_decay = jnp.prod(decay_in)
    lead_decay = jnp.cumprod(jnp.concatenate([jnp.ones((1,), jnp.float32), decay_in[:-1]]))
    piece = chunk // part_count
    extras = jnp.concatenate([octet_decay[None], pad])
    payload = jnp.concatenate(
        [
            octet_total.reshape(part_count, piece),
            jnp.broadcast_to(extras[None, :], (part_count, 128)),
        ],
        axis=1,
    )
    received = lax.all_to_all(payload, "ga", 0, 0, tiled=True)
    octet_in = jnp.dot(
        decay_weights(received[:, piece]), received[:, :piece], precision=highest_precision
    )
    octet_in = lax.all_to_all(octet_in, "ga", 0, 0, tiled=True).reshape(chunk)
    slices_out = local_in + lead_decay[:, None] * octet_in[None, :]
    carried_state = lax.all_to_all(slices_out, "gb", 0, 0, tiled=True).reshape(
        heads_here, key_width, value_width
    )

    vocab_rows = lax.all_gather(vocab_weight, "ga", axis=0, tiled=True)
    query_as_float = query_heads.astype(jnp.float32)
    state_contribution = (
        jnp.einsum("ugo,gow->ugw", query_as_float, carried_state, precision=highest_precision)
        * key_scaling
        * (jnp.exp(cumulative_decay) * continuation_flags[:, None].astype(jnp.float32))[:, :, None]
    )
    retained = in_block + state_contribution
    state_norms = jnp.log(
        1.0 + jnp.sqrt(jnp.mean(carried_state * carried_state, axis=(1, 2)) + 1e-06)
    )[None, :]
    normed = layer_norm(retained, 1e-06)
    gate_float = gate_proj.reshape(tok_count, heads_here, value_width).astype(jnp.float32)
    gated_out = (
        (normed * jax.nn.silu(gate_float))
        .astype(jnp.bfloat16)
        .reshape(tok_count, heads_here * value_width)
    )
    branch_parts = jnp.dot(gated_out, out_weight, preferred_element_type=jnp.float32)
    own_branch = jnp.sum(
        lax.all_to_all(
            branch_parts.reshape(head_count, slice_rows, -1), "head", 0, 0, tiled=True
        ),
        axis=0,
    )
    vocab_rows, own_branch = lax.optimization_barrier((vocab_rows, own_branch))
    stream = residual[0].astype(jnp.float32) + own_branch
    hidden = (layer_norm(stream, 1e-05) * norm_gain).astype(jnp.bfloat16)

    ga_index = lax.axis_index("ga")
    gb_index = lax.axis_index("gb")
    code = jnp.stack([targets[0] // 256, targets[0] % 256], axis=1).astype(jnp.bfloat16)
    hidden_ext = jnp.concatenate(
        [hidden, jnp.pad(code, ((0, 0), (0, 128 - code.shape[1])))], axis=1
    )
    spread = jnp.broadcast_to(hidden_ext[None], (sub,) + hidden_ext.shape)
    gathered = lax.all_gather(lax.all_to_all(spread, "gb", 0, 0, tiled=True), "head")
    width = hidden.shape[1]
    code_all = gathered[..., width : width + 2].astype(jnp.int32)
    all_targets = (code_all[..., 0] * 256 + code_all[..., 1]).reshape(-1)
    entry_ids = (
        (
            head_index * group_count
            + jnp.arange(part_count, dtype=jnp.int32)[:, None] * sub
            + gb_index
        )
        * vocab_here
        + jnp.arange(vocab_here, dtype=jnp.int32)[None, :]
    ).reshape(-1)
    logits = lax.dot_general(
        gathered[..., :width].reshape(-1, width),
        vocab_rows,
        (((1,), (1,)), ((), ())),
        preferred_element_type=jnp.float32,
    )
    top = jnp.max(logits, axis=1)
    exp_total = jnp.sum(jnp.exp(logits - top[:, None]), axis=1)
    picked = jnp.sum(jnp.where(entry_ids[None, :] == all_targets[:, None], logits, 0.0), axis=1)
    outgoing = jnp.stack([top, exp_total, picked]).reshape(3, head_count, sub, slice_rows)
    outgoing = jnp.transpose(outgoing, (1, 2, 0, 3)).reshape(head_count * sub, 3 * slice_rows)
    incoming = lax.all_to_all(outgoing, ("head", "gb"), 0, 0, tiled=True).reshape(
        head_count * sub, 3, slice_rows
    )
    own_max = jnp.max(incoming[:, 0], axis=0)
    own_total = jnp.sum(incoming[:, 1] * jnp.exp(incoming[:, 0] - own_max[None, :]), axis=0)
    own_target = jnp.sum(incoming[:, 2], axis=0)
    token_logp = own_target - own_max - jnp.log(own_total)
    token_ratio = response_mask[0].astype(jnp.float32) * (token_logp - ref_logp[0])
    own_positions = positions[0] + head_index * slice_rows + jnp.arange(slice_rows, dtype=jnp.int32)
    own_seq = jnp.sum((own_positions[:, None] >= starts[None, 1:]).astype(jnp.int32), axis=1)
    member = (own_seq[:, None] == jnp.arange(seq_count, dtype=jnp.int32)[None, :]).astype(
        jnp.float32
    )
    partial_sums = jnp.sum(member * token_ratio[:, None], axis=0)
    seq_total = partial_sums
    for axes in ("head", ("ga", "gb")):
        width = lax.axis_size(axes)
        spread = jnp.broadcast_to(seq_total[None, :], (width, seq_count))
        seq_total = jnp.sum(lax.all_to_all(spread, axes, 0, 0, tiled=True), axis=0)
    seq_ratio = seq_total / seq_lengths.astype(jnp.float32)
    return (seq_ratio, state_norms, own_max[None, :])


def decay_weights(decay):
    count = decay.shape[0]
    at = jnp.arange(count, dtype=jnp.int32)
    between = (at[None, None, :] > at[None, :, None]) & (at[None, None, :] < at[:, None, None])
    weights = jnp.prod(jnp.where(between, decay[None, None, :], 1.0), axis=2)
    return jnp.where(at[None, :] < at[:, None], weights, 0.0)


def solution(mesh):
    from jax.sharding import Mesh

    head_size, group_size = mesh.devices.shape
    sub = 8 if group_size % 8 == 0 else 1
    fine = Mesh(
        mesh.devices.reshape(head_size, group_size // sub, sub), ("head", "ga", "gb")
    )
    group = ("ga", "gb")
    placed = (
        P(group, "head"),
        P(group, "head"),
        P(group, "head"),
        P(group, "head"),
        P(group, "head"),
        P("head", None),
        P(group, "head", None),
        P(),
        P(("head", "ga", "gb"), None),
        P(group, "head"),
        P(group, "head"),
        P(group, "head"),
        P(),
    )
    return jax.shard_map(
        per_device,
        mesh=fine,
        in_specs=placed,
        out_specs=(P(), P(group, "head"), P(group, "head")),
        check_vma=False,
    )
```
